32 devices in a mesh: rep: 4 (over y, core), shard: 8 (over z, x).
Axes of the slice: x: 2, y: 2, z: 4, core: 2. Of those that a mesh axis runs over, the one named last changes fastest.
Arguments:
- cell_features: bfloat16 [4, 4096, 1024], P('rep', 'shard'), may hold values from -10 to 10
- upstream: bfloat16 [4, 4096, 1024], P('rep', 'shard'), may hold values from -0.119628906 to 0.119628906
- qkv_weight: bfloat16 [4, 1024, 3072], P('rep', 'shard'), may hold values from -0.1875 to 0.1875
- out_weight: bfloat16 [4, 1024, 1024], P('rep', 'shard'), may hold values from -0.1875 to 0.1875
- momentum: float32 [4, 1024, 1024], P('rep', 'shard'), may hold values from -4 to 4
- key_tiles: int32 [4, 32, 6], P('rep'), may hold values from 0 to 31, as said below
- live_blocks: int32 [4, 32], P('rep'), may hold values from 1 to 6
- step_index: int32 [], replicated, may hold values from 0 to 999
Outputs:
- layer_out: bfloat16 [4, 4096, 1024], P('rep', 'shard')
- new_weight: bfloat16 [4, 1024, 1024], P('rep', 'shard')
- new_momentum: float32 [4, 1024, 1024], P('rep', 'shard')
The draws below stay inside these ranges and needn't reach their ends.
Inputs may be any that keep to these rules, and one draw needn't show every extreme that they name: `key_tiles`: every entry names a tile of its group. Of the 24 entries of device d's 4 query tiles (tiles d*4 to (d+1)*4 - 1), exactly 12 name tiles of device d itself (tile // 4 == d); of the others at most 2 name tiles of any one other device, and in every draw some device is named exactly 2 times.
All inputs are finite; a program needn't handle non-finite values.
Results may differ from the reference program's by a relative error of at most 0.025.
Values may be sent and summed in bfloat16 or wider, within the bound.
No kernel may reach another device: no remote copies, remote signals or barrier semaphores. Data moves between devices by JAX's collectives and lax.ppermute only.
A program may use at most 128 MiB of HBM per device.

```python
import jax
import jax.numpy as jnp
from jax import lax

D = 1024
HEADS = 16
HEAD_DIM = 64
TILE = 128
KB = 6
TILES_DEV = 4
GTILES = 32
CELLS = 4096
REPLICAS = 4
LOCAL = 12
REMOTE = 12
CAP = 2
N_REP = 4
N_SHARD = 8


def draw_cell_features(key, part):
    first_key = jax.random.fold_in(key, 0)
    base = jax.random.normal(first_key, (REPLICAS, CELLS, D), jnp.float32)
    return jnp.clip(base, -10.0, 10.0).astype(jnp.bfloat16)


def draw_key_tiles(key, part):
    device_keys = jax.random.split(jax.random.fold_in(key, 7), N_REP * N_SHARD)
    device_numbers = jnp.arange(N_REP * N_SHARD, dtype=jnp.int32) % N_SHARD

    def one_device(device_key, device):
        perm_key, shuffle_key, tile_key, local_key = jax.random.split(device_key, 4)
        others = jnp.arange(1, N_SHARD, dtype=jnp.int32)
        perms = jax.vmap(lambda inner: jax.random.permutation(inner, others))(jax.random.split(perm_key, CAP))
        offsets = perms.reshape(-1)[:REMOTE]
        owners = (device + offsets) % N_SHARD
        remote_tiles = owners * TILES_DEV + jax.random.randint(tile_key, (REMOTE,), 0, TILES_DEV)
        local_tiles = device * TILES_DEV + jax.random.randint(local_key, (LOCAL,), 0, TILES_DEV)
        entries = jnp.concatenate([local_tiles, remote_tiles]).astype(jnp.int32)
        return jax.random.permutation(shuffle_key, entries).astype(jnp.int32)
    return jax.vmap(one_device)(device_keys, device_numbers).reshape(N_REP, N_SHARD * TILES_DEV, KB)


def plant(array, rng, smallest, largest):
    longest = array.shape.index(max(array.shape))
    spots = []
    for shift in (0, 1):
        where = [jax.random.randint(jax.random.fold_in(rng, axis), (), 0, length) for axis, length in enumerate(array.shape)]
        where[longest] = (where[longest] + shift) % array.shape[longest]
        spots.append(tuple(where))
    return array.at[spots[0]].set(smallest).at[spots[1]].set(largest)


def level_of(key, shape, cuts, low, largest):
    level, own = 1.0, jax.random.fold_in(key, 6)
    for axis_at, parts in cuts:
        steps = jnp.exp(jax.random.uniform(jax.random.fold_in(own, axis_at), (parts,), jnp.float32, low / len(cuts), largest / len(cuts)))
        level = level * jnp.repeat(steps, shape[axis_at] // parts).reshape([-1 if axis == axis_at else 1 for axis in range(len(shape))])
    return level


def centred(key, shape, scale, bound, shards=(), held_as=jnp.bfloat16):
    result = jax.random.normal(key, shape, jnp.float32) * scale
    if len(shards) > 0:
        result = level_of(key, shape, shards, -0.22, 0.18) * result
    return jnp.clip(result, min=-bound, max=bound).astype(held_as)


def setup_inputs(seed: int = 0) -> dict:
    splits = jax.random.split(jax.random.key(seed), 9)
    return {
        "cell_features": draw_cell_features(jax.random.fold_in(splits[8], 71), 0),
        "upstream": centred(splits[1], (REPLICAS, CELLS, D), 0.02, 0.119628906, ((0, 4), (1, 8))),
        "qkv_weight": centred(splits[2], (REPLICAS, D, 3 * D), D ** -0.5, 0.1875, ((0, 4), (1, 8))),
        "out_weight": centred(splits[3], (REPLICAS, D, D), D ** -0.5, 0.1875, ((0, 4), (1, 8))),
        "momentum": centred(splits[4], (REPLICAS, D, D), 0.5, 4.0, ((0, 4), (1, 8)), jnp.float32),
        "key_tiles": draw_key_tiles(jax.random.fold_in(splits[8], 71), 0),
        "live_blocks": plant(jax.random.randint(splits[6], (REPLICAS, GTILES), 1, KB + 1), jax.random.fold_in(splits[6], 1), 1, KB).astype(jnp.int32),
        "step_index": jax.random.randint(splits[7], (), 0, 1000).astype(jnp.int32),
    }


momentum_beta = 0.9


def attend_tile(query_tile, key_value, live_count):
    model_width = query_tile.shape[1]
    query_split = query_tile.reshape(TILE, HEADS, HEAD_DIM).astype(jnp.float32)
    keys_split = key_value[:, :model_width].reshape(KB * TILE, HEADS, HEAD_DIM).astype(jnp.float32)
    values_split = key_value[:, model_width:].reshape(KB * TILE, HEADS, HEAD_DIM).astype(jnp.float32)
    scores = jnp.einsum("qhd,khd->hqk", query_split, keys_split) * (HEAD_DIM ** -0.5)
    usable = (jnp.arange(KB * TILE, dtype=jnp.int32) // TILE) < live_count
    scores = jnp.where(usable[None, None, :], scores, jnp.float32(-1e30))
    row_max = jnp.max(scores, axis=2, keepdims=True)
    exponent = jnp.exp(scores - row_max)
    probabilities = (exponent / jnp.sum(exponent, axis=2, keepdims=True)).astype(jnp.bfloat16)
    mixture = jnp.einsum("hqk,khd->qhd", probabilities.astype(jnp.float32), values_split)
    return mixture.reshape(TILE, model_width).astype(jnp.bfloat16)


def replica_step(inputs, learn_rate):
    features, cotangent, qkv, weight, moment, tile_lists, live = inputs
    projected = jnp.dot(features, qkv, preferred_element_type=jnp.float32).astype(jnp.bfloat16)
    query = projected[:, :D].reshape(GTILES, TILE, D)
    key_value = projected[:, D:].reshape(GTILES, TILE, 2 * D)

    def one_tile(element):
        query_tile, listed, live_count = element
        gathered = key_value[listed].reshape(KB * TILE, 2 * D)
        return attend_tile(query_tile, gathered, live_count)

    attended = lax.map(one_tile, (query, tile_lists, live)).reshape(CELLS, D)
    product = jnp.dot(attended, weight, preferred_element_type=jnp.float32)
    layer_out = (features.astype(jnp.float32) + product).astype(jnp.bfloat16)
    gradient = jnp.dot(attended.T, cotangent, preferred_element_type=jnp.float32)
    velocity = momentum_beta * moment + gradient
    stepped = (weight.astype(jnp.float32) - learn_rate * velocity).astype(jnp.bfloat16)
    return layer_out, stepped, velocity


def reference(cell_features, upstream, qkv_weight, out_weight, momentum, key_tiles, live_blocks, step_index):
    learn_rate = jnp.float32(50.0) / (jnp.float32(500.0) + step_index.astype(jnp.float32))
    layer_out, stepped, velocity = lax.map(lambda inputs: replica_step(inputs, learn_rate), (cell_features, upstream, qkv_weight, out_weight, momentum, key_tiles, live_blocks))
    bit_count = N_REP.bit_length() - 1
    bit_number = (step_index % bit_count).astype(jnp.int32)
    partner = jnp.bitwise_xor(jnp.arange(N_REP, dtype=jnp.int32), jnp.left_shift(jnp.int32(1), bit_number).astype(jnp.int32))
    new_weight = (0.5 * (stepped.astype(jnp.float32) + stepped[partner].astype(jnp.float32))).astype(jnp.bfloat16)
    new_momentum = 0.5 * (velocity + velocity[partner])
    return layer_out, new_weight, new_momentum
```

```python
import functools

import jax
import jax.numpy as jnp
from jax import lax
from jax.experimental import pallas as pl
from jax.experimental.pallas import tpu as pltpu
from jax.sharding import PartitionSpec as P

HEADS = 16
HEAD_DIM = 64
TILE = 128
KB = 6


momentum_beta = 0.9


def shortened(value):

    def short(part):
        return part.astype(jnp.bfloat16) if part.dtype == jnp.float32 else part

    return jax.tree.map(short, value)


def partner(value, axis, bit):
    return lax.ppermute(value, axis, [(i, i ^ 1 << bit) for i in range(lax.axis_size(axis))])


def add_rows(source, shard_rows):
    return jnp.dot(source, shard_rows, preferred_element_type=jnp.float32)


def attention_kernel(index_ref, live_ref, query_ref, *refs):
    kv_refs = refs[:KB]
    out_ref = refs[KB]
    tile = pl.program_id(0)
    live = live_ref[tile]
    model_width = query_ref.shape[1]
    pair_width = 2 * HEAD_DIM
    lane = lax.broadcasted_iota(jnp.int32, (TILE, pair_width), 1)
    first_half = lane < HEAD_DIM
    slot_of = lax.broadcasted_iota(jnp.int32, (TILE, KB * TILE), 1) // TILE
    usable = slot_of < live
    for pair in range(HEADS // 2):
        lo = pair * pair_width
        query_pair = query_ref[:, lo:lo + pair_width]
        keys = [kv_refs[j][0, :, lo:lo + pair_width] for j in range(KB)]
        values = [kv_refs[j][0, :, model_width + lo:model_width + lo + pair_width] for j in range(KB)]
        outs = []
        for half in range(2):
            keep = first_half if half == 0 else jnp.logical_not(first_half)
            query_head = jnp.where(keep, query_pair, jnp.zeros_like(query_pair))
            scores = jnp.concatenate(
                [
                    lax.dot_general(
                        query_head, keys[j], (((1,), (1,)), ((), ())),
                        preferred_element_type=jnp.float32,
                    )
                    for j in range(KB)
                ],
                axis=1,
            ) * jnp.float32(HEAD_DIM ** (-0.5))
            scores = jnp.where(usable, scores, jnp.float32(-1e30))
            row_max = jnp.max(scores, axis=1, keepdims=True)
            exponent = jnp.exp(scores - row_max)
            probabilities = (exponent / jnp.sum(exponent, axis=1, keepdims=True)).astype(jnp.bfloat16)
            mixture = jnp.zeros((TILE, pair_width), jnp.float32)
            for j in range(KB):
                mixture = mixture + jnp.dot(
                    probabilities[:, j * TILE:(j + 1) * TILE], values[j],
                    preferred_element_type=jnp.float32,
                )
            outs.append(mixture)
        joined = jnp.where(first_half, outs[0], outs[1])
        out_ref[:, lo:lo + pair_width] = joined.astype(out_ref.dtype)


def attend(query, kv_table, slot_index, live_mine):
    row_count, model_width = query.shape
    tile_count = row_count // TILE

    def kv_spec(j):
        return pl.BlockSpec(
            (1, TILE, 2 * model_width), lambda t, idx, live: (idx[t * KB + j], 0, 0)
        )

    grid_spec = pltpu.PrefetchScalarGridSpec(
        num_scalar_prefetch=2,
        grid=(tile_count,),
        in_specs=[pl.BlockSpec((TILE, model_width), lambda t, idx, live: (t, 0))]
        + [kv_spec(j) for j in range(KB)],
        out_specs=pl.BlockSpec((TILE, model_width), lambda t, idx, live: (t, 0)),
    )
    return pl.pallas_call(
        attention_kernel,
        grid_spec=grid_spec,
        out_shape=jax.ShapeDtypeStruct((row_count, model_width), jnp.bfloat16),
        compiler_params=pltpu.CompilerParams(dimension_semantics=("arbitrary",)),
    )(slot_index, live_mine, query, *([kv_table] * KB))


def swap_with(bit_number, stacked_pair):
    return jax.tree.map(
        lambda part, own: part.astype(own.dtype),
        partner(shortened(stacked_pair), "rep", bit_number),
        stacked_pair,
    )


def body(
    cell_features, upstream, qkv_weight, out_weight, momentum, key_tiles, live_blocks, step_index
):
    features = cell_features[0]
    row_count, model_width = features.shape
    tile_count = row_count // TILE
    shard_count = lax.axis_size("shard")
    my_index = lax.axis_index("shard")
    slot_count = tile_count * KB
    remote_count = slot_count - slot_count // 2
    capacity = (remote_count + shard_count - 2) // (shard_count - 1)
    requests = key_tiles[0].reshape(shard_count, slot_count)
    owners = requests // tile_count
    local_tile = requests % tile_count
    positions = jnp.arange(slot_count, dtype=jnp.int32)
    earlier = positions[None, :] < positions[:, None]
    same_owner = owners[:, :, None] == owners[:, None, :]
    owner_rank = jnp.sum((same_owner & earlier[None]).astype(jnp.int32), axis=2)
    offsets = jnp.arange(1, shard_count, dtype=jnp.int32)
    receivers = (my_index + offsets) % shard_count
    their_owners = owners[receivers]
    their_ranks = owner_rank[receivers]
    their_local = local_tile[receivers]
    slot_ids = jnp.arange(capacity, dtype=jnp.int32)
    chosen = ((their_owners == my_index)[:, :, None]) & (their_ranks[:, :, None] == slot_ids[None, None, :])
    send_index = jnp.sum(chosen.astype(jnp.int32) * their_local[:, :, None], axis=1)
    feature_tiles = features.reshape(tile_count, TILE, model_width)
    outgoing = feature_tiles[send_index.reshape(-1)].reshape(
        shard_count - 1, capacity, TILE, model_width
    )
    arrived = [
        lax.ppermute(
            outgoing[k - 1],
            "shard",
            [(i, (i + k) % shard_count) for i in range(shard_count)],
        )
        for k in range(1, shard_count)
    ]
    arrived_rows = jnp.concatenate(arrived, axis=0).reshape(-1, model_width)
    my_owners = lax.dynamic_index_in_dim(owners, my_index, 0, keepdims=False)
    my_ranks = lax.dynamic_index_in_dim(owner_rank, my_index, 0, keepdims=False)
    my_local = lax.dynamic_index_in_dim(local_tile, my_index, 0, keepdims=False)
    my_remote = my_owners != my_index
    my_offset = (my_index - my_owners) % shard_count
    table_size = tile_count + (shard_count - 1) * capacity
    slot_index = jnp.where(my_remote, tile_count + (my_offset - 1) * capacity + my_ranks, my_local)
    slot_index = jnp.clip(slot_index, 0, table_size - 1).astype(jnp.int32)
    full_qkv = lax.all_gather(qkv_weight[0], "shard", axis=0, tiled=True)
    query = add_rows(features, full_qkv[:, :model_width]).astype(jnp.bfloat16)
    kv_table = add_rows(
        jnp.concatenate([features, arrived_rows], axis=0), full_qkv[:, model_width:]
    ).astype(jnp.bfloat16).reshape(table_size, TILE, 2 * model_width)
    live_mine = lax.dynamic_slice_in_dim(live_blocks[0], my_index * tile_count, tile_count, 0)
    attended = attend(query, kv_table, slot_index, live_mine.astype(jnp.int32))
    product = add_rows(attended, lax.all_gather(out_weight[0], "shard", axis=0, tiled=True))
    layer_out = (features.astype(jnp.float32) + product).astype(jnp.bfloat16)
    gradient = lax.psum_scatter(
        lax.dot_general(
            attended, upstream[0], (((0,), (0,)), ((), ())), preferred_element_type=jnp.float32
        ).astype(jnp.bfloat16),
        "shard",
        scatter_dimension=0,
        tiled=True,
    ).astype(jnp.float32)
    learn_rate = jnp.float32(50.0) / (jnp.float32(500.0) + step_index.astype(jnp.float32))
    velocity = momentum_beta * momentum[0] + gradient
    stepped = (out_weight[0].astype(jnp.float32) - learn_rate * velocity).astype(jnp.bfloat16)
    stacked_pair = jnp.stack([stepped.astype(jnp.float32), velocity])
    bit_count = lax.axis_size("rep").bit_length() - 1
    branches = [functools.partial(swap_with, bit_number) for bit_number in range(bit_count)]
    bit_choice = step_index % bit_count
    partner_pair = lax.switch(bit_choice, branches, stacked_pair)
    averaged = 0.5 * (stacked_pair + partner_pair)
    new_weight = averaged[0].astype(jnp.bfloat16)
    new_momentum = averaged[1]
    return (layer_out[None], new_weight[None], new_momentum[None])


def solution(mesh):
    placed = (
        P("rep", "shard", None),
        P("rep", "shard", None),
        P("rep", "shard", None),
        P("rep", "shard", None),
        P("rep", "shard", None),
        P("rep", None, None),
        P("rep", None),
        P(),
    )
    return jax.shard_map(
        body,
        mesh=mesh,
        in_specs=placed,
        out_specs=(P("rep", "shard", None), P("rep", "shard", None), P("rep", "shard", None)),
        check_vma=False,
    )
```

```python
import functools

import jax
import jax.numpy as jnp
from jax import lax
from jax.experimental import pallas as pl
from jax.experimental.pallas import tpu as pltpu
from jax.sharding import PartitionSpec as P

HEADS = 16
HEAD_DIM = 64
TILE = 128
KB = 6


momentum_beta = 0.9


def shortened(value):

    def short(part):
        return part.astype(jnp.bfloat16) if part.dtype == jnp.float32 else part

    return jax.tree.map(short, value)


def partner(value, axis, bit):
    return lax.ppermute(value, axis, [(i, i ^ 1 << bit) for i in range(lax.axis_size(axis))])


def add_rows(source, shard_rows):
    return jnp.dot(source, shard_rows, preferred_element_type=jnp.float32)


def attention_kernel(index_ref, live_ref, query_ref, *refs):
    kv_refs = refs[:KB]
    out_ref = refs[KB]
    tile = pl.program_id(0)
    live = live_ref[tile]
    model_width = query_ref.shape[1]
    pair_width = 2 * HEAD_DIM
    lane = lax.broadcasted_iota(jnp.int32, (TILE, pair_width), 1)
    first_half = lane < HEAD_DIM
    slot_of = lax.broadcasted_iota(jnp.int32, (TILE, KB * TILE), 1) // TILE
    usable = slot_of < live
    for pair in range(HEADS // 2):
        lo = pair * pair_width
        query_pair = query_ref[:, lo:lo + pair_width]
        keys = [kv_refs[j][0, :, lo:lo + pair_width] for j in range(KB)]
        values = [kv_refs[j][0, :, model_width + lo:model_width + lo + pair_width] for j in range(KB)]
        outs = []
        for half in range(2):
            keep = first_half if half == 0 else jnp.logical_not(first_half)
            query_head = jnp.where(keep, query_pair, jnp.zeros_like(query_pair))
            scores = jnp.concatenate(
                [
                    lax.dot_general(
                        query_head, keys[j], (((1,), (1,)), ((), ())),
                        preferred_element_type=jnp.float32,
                    )
                    for j in range(KB)
                ],
                axis=1,
            ) * jnp.float32(HEAD_DIM ** (-0.5))
            scores = jnp.where(usable, scores, jnp.float32(-1e30))
            row_max = jnp.max(scores, axis=1, keepdims=True)
            exponent = jnp.exp(scores - row_max)
            probabilities = (exponent / jnp.sum(exponent, axis=1, keepdims=True)).astype(jnp.bfloat16)
            mixture = jnp.zeros((TILE, pair_width), jnp.float32)
            for j in range(KB):
                mixture = mixture + jnp.dot(
                    probabilities[:, j * TILE:(j + 1) * TILE], values[j],
                    preferred_element_type=jnp.float32,
                )
            outs.append(mixture)
        joined = jnp.where(first_half, outs[0], outs[1])
        out_ref[:, lo:lo + pair_width] = joined.astype(out_ref.dtype)


def attend(query, kv_table, slot_index, live_mine):
    row_count, model_width = query.shape
    tile_count = row_count // TILE

    def kv_spec(j):
        return pl.BlockSpec(
            (1, TILE, 2 * model_width), lambda t, idx, live: (idx[t * KB + j], 0, 0)
        )

    grid_spec = pltpu.PrefetchScalarGridSpec(
        num_scalar_prefetch=2,
        grid=(tile_count,),
        in_specs=[pl.BlockSpec((TILE, model_width), lambda t, idx, live: (t, 0))]
        + [kv_spec(j) for j in range(KB)],
        out_specs=pl.BlockSpec((TILE, model_width), lambda t, idx, live: (t, 0)),
    )
    return pl.pallas_call(
        attention_kernel,
        grid_spec=grid_spec,
        out_shape=jax.ShapeDtypeStruct((row_count, model_width), jnp.bfloat16),
        compiler_params=pltpu.CompilerParams(dimension_semantics=("arbitrary",)),
    )(slot_index, live_mine, query, *([kv_table] * KB))


def pick_partner(bit_choice, bit_count, value):
    candidates = [partner(value, "rep", bit_number) for bit_number in range(bit_count)]
    return jax.tree.map(
        lambda *parts: lax.select_n(bit_choice, *parts) if len(parts) > 1 else parts[0],
        *candidates,
    )


def body(
    cell_features, upstream, qkv_weight, out_weight, momentum, key_tiles, live_blocks, step_index
):
    features = cell_features[0]
    row_count, model_width = features.shape
    tile_count = row_count // TILE
    shard_count = lax.axis_size("shard")
    my_index = lax.axis_index("shard")
    slot_count = tile_count * KB
    remote_count = slot_count - slot_count // 2
    capacity = (remote_count + shard_count - 2) // (shard_count - 1)
    requests = key_tiles[0].reshape(shard_count, slot_count)
    owners = requests // tile_count
    local_tile = requests % tile_count
    positions = jnp.arange(slot_count, dtype=jnp.int32)
    earlier = positions[None, :] < positions[:, None]
    same_owner = owners[:, :, None] == owners[:, None, :]
    owner_rank = jnp.sum((same_owner & earlier[None]).astype(jnp.int32), axis=2)
    offsets = jnp.arange(1, shard_count, dtype=jnp.int32)
    receivers = (my_index + offsets) % shard_count
    their_owners = owners[receivers]
    their_ranks = owner_rank[receivers]
    their_local = local_tile[receivers]
    slot_ids = jnp.arange(capacity, dtype=jnp.int32)
    chosen = ((their_owners == my_index)[:, :, None]) & (their_ranks[:, :, None] == slot_ids[None, None, :])
    send_index = jnp.sum(chosen.astype(jnp.int32) * their_local[:, :, None], axis=1)
    feature_tiles = features.reshape(tile_count, TILE, model_width)
    outgoing = feature_tiles[send_index.reshape(-1)].reshape(
        shard_count - 1, capacity, TILE, model_width
    )
    arrived = [
        lax.ppermute(
            outgoing[k - 1],
            "shard",
            [(i, (i + k) % shard_count) for i in range(shard_count)],
        )
        for k in range(1, shard_count)
    ]
    arrived_rows = jnp.concatenate(arrived, axis=0).reshape(-1, model_width)
    bit_count = lax.axis_size("rep").bit_length() - 1
    bit_choice = step_index % bit_count
    own_weight = out_weight[0]
    own_moment = momentum[0]
    their_weight, their_moment = pick_partner(bit_choice, bit_count, (own_weight, own_moment))
    arrived_rows, their_weight, their_moment = lax.optimization_barrier(
        (arrived_rows, their_weight, their_moment)
    )
    my_owners = lax.dynamic_index_in_dim(owners, my_index, 0, keepdims=False)
    my_ranks = lax.dynamic_index_in_dim(owner_rank, my_index, 0, keepdims=False)
    my_local = lax.dynamic_index_in_dim(local_tile, my_index, 0, keepdims=False)
    my_remote = my_owners != my_index
    my_offset = (my_index - my_owners) % shard_count
    table_size = tile_count + (shard_count - 1) * capacity
    slot_index = jnp.where(my_remote, tile_count + (my_offset - 1) * capacity + my_ranks, my_local)
    slot_index = jnp.clip(slot_index, 0, table_size - 1).astype(jnp.int32)
    full_qkv = lax.all_gather(qkv_weight[0], "shard", axis=0, tiled=True)
    query = add_rows(features, full_qkv[:, :model_width]).astype(jnp.bfloat16)
    kv_table = add_rows(
        jnp.concatenate([features, arrived_rows], axis=0), full_qkv[:, model_width:]
    ).astype(jnp.bfloat16).reshape(table_size, TILE, 2 * model_width)
    live_mine = lax.dynamic_slice_in_dim(live_blocks[0], my_index * tile_count, tile_count, 0)
    attended = attend(query, kv_table, slot_index, live_mine.astype(jnp.int32))
    product = add_rows(attended, lax.all_gather(out_weight[0], "shard", axis=0, tiled=True))
    layer_out = (features.astype(jnp.float32) + product).astype(jnp.bfloat16)
    partial = lax.dot_general(
        attended, upstream[0], (((0,), (0,)), ((), ())), preferred_element_type=jnp.float32
    ).astype(jnp.bfloat16)
    block_rows = partial.shape[0] // shard_count
    blocks = partial.reshape(shard_count, block_rows, partial.shape[1])
    gradient = lax.dynamic_index_in_dim(blocks, my_index, 0, keepdims=False).astype(jnp.float32)
    for k in range(1, shard_count):
        piece = lax.dynamic_index_in_dim(blocks, (my_index + k) % shard_count, 0, keepdims=False)
        gradient = gradient + lax.ppermute(
            piece, "shard", [(i, (i + k) % shard_count) for i in range(shard_count)]
        ).astype(jnp.float32)
    learn_rate = jnp.float32(50.0) / (jnp.float32(500.0) + step_index.astype(jnp.float32))
    their_gradient = pick_partner(bit_choice, bit_count, gradient.astype(jnp.bfloat16))
    velocity = momentum_beta * own_moment + gradient
    their_velocity = momentum_beta * their_moment + their_gradient.astype(jnp.float32)
    stepped = (own_weight.astype(jnp.float32) - learn_rate * velocity).astype(jnp.bfloat16)
    their_stepped = (
        their_weight.astype(jnp.float32) - learn_rate * their_velocity
    ).astype(jnp.bfloat16)
    new_weight = (
        0.5 * (stepped.astype(jnp.float32) + their_stepped.astype(jnp.float32))
    ).astype(jnp.bfloat16)
    new_momentum = 0.5 * (velocity + their_velocity)
    return (layer_out[None], new_weight[None], new_momentum[None])


def solution(mesh):
    placed = (
        P("rep", "shard", None),
        P("rep", "shard", None),
        P("rep", "shard", None),
        P("rep", "shard", None),
        P("rep", "shard", None),
        P("rep", None, None),
        P("rep", None),
        P(),
    )
    return jax.shard_map(
        body,
        mesh=mesh,
        in_specs=placed,
        out_specs=(P("rep", "shard", None), P("rep", "shard", None), P("rep", "shard", None)),
        check_vma=False,
    )
```

```python
import functools

import jax
import jax.numpy as jnp
from jax import lax
from jax.experimental import pallas as pl
from jax.experimental.pallas import tpu as pltpu
from jax.sharding import PartitionSpec as P

HEADS = 16
HEAD_DIM = 64
TILE = 128
KB = 6


momentum_beta = 0.9


def shortened(value):

    def short(part):
        return part.astype(jnp.bfloat16) if part.dtype == jnp.float32 else part

    return jax.tree.map(short, value)


def partner(value, axis, bit):
    return lax.ppermute(value, axis, [(i, i ^ 1 << bit) for i in range(lax.axis_size(axis))])


def add_rows(source, shard_rows):
    return jnp.dot(source, shard_rows, preferred_element_type=jnp.float32)


def attention_kernel(index_ref, live_ref, query_ref, *refs):
    kv_refs = refs[:KB]
    out_ref = refs[KB]
    tile = pl.program_id(0)
    live = live_ref[tile]
    model_width = query_ref.shape[1]
    pair_width = 2 * HEAD_DIM
    lane = lax.broadcasted_iota(jnp.int32, (TILE, pair_width), 1)
    first_half = lane < HEAD_DIM
    slot_of = lax.broadcasted_iota(jnp.int32, (TILE, KB * TILE), 1) // TILE
    usable = slot_of < live
    for pair in range(HEADS // 2):
        lo = pair * pair_width
        query_pair = query_ref[:, lo:lo + pair_width]
        keys = [kv_refs[j][0, :, lo:lo + pair_width] for j in range(KB)]
        values = [kv_refs[j][0, :, model_width + lo:model_width + lo + pair_width] for j in range(KB)]
        outs = []
        for half in range(2):
            keep = first_half if half == 0 else jnp.logical_not(first_half)
            query_head = jnp.where(keep, query_pair, jnp.zeros_like(query_pair))
            scores = jnp.concatenate(
                [
                    lax.dot_general(
                        query_head, keys[j], (((1,), (1,)), ((), ())),
                        preferred_element_type=jnp.float32,
                    )
                    for j in range(KB)
                ],
                axis=1,
            ) * jnp.float32(HEAD_DIM ** (-0.5))
            scores = jnp.where(usable, scores, jnp.float32(-1e30))
            row_max = jnp.max(scores, axis=1, keepdims=True)
            exponent = jnp.exp(scores - row_max)
            inverse = 1.0 / jnp.sum(exponent, axis=1, keepdims=True)
            weights = exponent.astype(jnp.bfloat16)
            mixture = jnp.zeros((TILE, pair_width), jnp.float32)
            for j in range(KB):
                mixture = mixture + jnp.dot(
                    weights[:, j * TILE:(j + 1) * TILE], values[j],
                    preferred_element_type=jnp.float32,
                )
            mixture = mixture * inverse
            outs.append(mixture)
        joined = jnp.where(first_half, outs[0], outs[1])
        out_ref[:, lo:lo + pair_width] = joined.astype(out_ref.dtype)


def attend(query, kv_table, slot_index, live_mine):
    row_count, model_width = query.shape
    tile_count = row_count // TILE

    def kv_spec(j):
        return pl.BlockSpec(
            (1, TILE, 2 * model_width), lambda t, idx, live: (idx[t * KB + j], 0, 0)
        )

    grid_spec = pltpu.PrefetchScalarGridSpec(
        num_scalar_prefetch=2,
        grid=(tile_count,),
        in_specs=[pl.BlockSpec((TILE, model_width), lambda t, idx, live: (t, 0))]
        + [kv_spec(j) for j in range(KB)],
        out_specs=pl.BlockSpec((TILE, model_width), lambda t, idx, live: (t, 0)),
    )
    return pl.pallas_call(
        attention_kernel,
        grid_spec=grid_spec,
        out_shape=jax.ShapeDtypeStruct((row_count, model_width), jnp.bfloat16),
        compiler_params=pltpu.CompilerParams(dimension_semantics=("arbitrary",)),
    )(slot_index, live_mine, query, *([kv_table] * KB))


def pick_partner(bit_choice, bit_count, value):
    candidates = [partner(value, "rep", bit_number) for bit_number in range(bit_count)]
    return jax.tree.map(
        lambda *parts: lax.select_n(bit_choice, *parts) if len(parts) > 1 else parts[0],
        *candidates,
    )


def body(
    cell_features, upstream, qkv_weight, out_weight, momentum, key_tiles, live_blocks, step_index
):
    features = cell_features[0]
    row_count, model_width = features.shape
    tile_count = row_count // TILE
    shard_count = lax.axis_size("shard")
    my_index = lax.axis_index("shard")
    slot_count = tile_count * KB
    remote_count = slot_count - slot_count // 2
    capacity = (remote_count + shard_count - 2) // (shard_count - 1)
    requests = key_tiles[0].reshape(shard_count, slot_count)
    owners = requests // tile_count
    local_tile = requests % tile_count
    positions = jnp.arange(slot_count, dtype=jnp.int32)
    earlier = positions[None, :] < positions[:, None]
    same_owner = owners[:, :, None] == owners[:, None, :]
    owner_rank = jnp.sum((same_owner & earlier[None]).astype(jnp.int32), axis=2)
    offsets = jnp.arange(1, shard_count, dtype=jnp.int32)
    receivers = (my_index + offsets) % shard_count
    their_owners = owners[receivers]
    their_ranks = owner_rank[receivers]
    their_local = local_tile[receivers]
    slot_ids = jnp.arange(capacity, dtype=jnp.int32)
    chosen = ((their_owners == my_index)[:, :, None]) & (their_ranks[:, :, None] == slot_ids[None, None, :])
    send_index = jnp.sum(chosen.astype(jnp.int32) * their_local[:, :, None], axis=1)
    feature_tiles = features.reshape(tile_count, TILE, model_width)
    outgoing = feature_tiles[send_index.reshape(-1)].reshape(
        shard_count - 1, capacity, TILE, model_width
    )
    arrived = [
        lax.ppermute(
            outgoing[k - 1],
            "shard",
            [(i, (i + k) % shard_count) for i in range(shard_count)],
        )
        for k in range(1, shard_count)
    ]
    arrived_rows = jnp.concatenate(arrived, axis=0).reshape(-1, model_width)
    bit_count = lax.axis_size("rep").bit_length() - 1
    bit_choice = step_index % bit_count
    own_weight = out_weight[0]
    own_moment = momentum[0]
    their_weight, their_moment = pick_partner(bit_choice, bit_count, (own_weight, own_moment))
    arrived_rows, their_weight, their_moment = lax.optimization_barrier(
        (arrived_rows, their_weight, their_moment)
    )
    my_owners = lax.dynamic_index_in_dim(owners, my_index, 0, keepdims=False)
    my_ranks = lax.dynamic_index_in_dim(owner_rank, my_index, 0, keepdims=False)
    my_local = lax.dynamic_index_in_dim(local_tile, my_index, 0, keepdims=False)
    my_remote = my_owners != my_index
    my_offset = (my_index - my_owners) % shard_count
    table_size = tile_count + (shard_count - 1) * capacity
    slot_index = jnp.where(my_remote, tile_count + (my_offset - 1) * capacity + my_ranks, my_local)
    slot_index = jnp.clip(slot_index, 0, table_size - 1).astype(jnp.int32)
    full_qkv = lax.all_gather(qkv_weight[0], "shard", axis=0, tiled=True)
    query = add_rows(features, full_qkv[:, :model_width]).astype(jnp.bfloat16)
    kv_table = add_rows(
        jnp.concatenate([features, arrived_rows], axis=0), full_qkv[:, model_width:]
    ).astype(jnp.bfloat16).reshape(table_size, TILE, 2 * model_width)
    live_mine = lax.dynamic_slice_in_dim(live_blocks[0], my_index * tile_count, tile_count, 0)
    attended = attend(query, kv_table, slot_index, live_mine.astype(jnp.int32))
    product = add_rows(attended, lax.all_gather(out_weight[0], "shard", axis=0, tiled=True))
    layer_out = (features.astype(jnp.float32) + product).astype(jnp.bfloat16)
    partial = lax.dot_general(
        attended, upstream[0], (((0,), (0,)), ((), ())), preferred_element_type=jnp.float32
    ).astype(jnp.bfloat16)
    block_rows = partial.shape[0] // shard_count
    blocks = partial.reshape(shard_count, block_rows, partial.shape[1])
    gradient = lax.dynamic_index_in_dim(blocks, my_index, 0, keepdims=False).astype(jnp.float32)
    for k in range(1, shard_count):
        piece = lax.dynamic_index_in_dim(blocks, (my_index + k) % shard_count, 0, keepdims=False)
        received = lax.ppermute(
            piece, "shard", [(i, (i + k) % shard_count) for i in range(shard_count)]
        )
        if k == 1:
            received, layer_out = lax.optimization_barrier((received, layer_out))
        gradient = gradient + received.astype(jnp.float32)
    learn_rate = jnp.float32(50.0) / (jnp.float32(500.0) + step_index.astype(jnp.float32))
    their_gradient = pick_partner(bit_choice, bit_count, gradient.astype(jnp.bfloat16))
    velocity = momentum_beta * own_moment + gradient
    their_velocity = momentum_beta * their_moment + their_gradient.astype(jnp.float32)
    stepped = (own_weight.astype(jnp.float32) - learn_rate * velocity).astype(jnp.bfloat16)
    their_stepped = (
        their_weight.astype(jnp.float32) - learn_rate * their_velocity
    ).astype(jnp.bfloat16)
    new_weight = (
        0.5 * (stepped.astype(jnp.float32) + their_stepped.astype(jnp.float32))
    ).astype(jnp.bfloat16)
    new_momentum = 0.5 * (velocity + their_velocity)
    return (layer_out[None], new_weight[None], new_momentum[None])


def solution(mesh):
    placed = (
        P("rep", "shard", None),
        P("rep", "shard", None),
        P("rep", "shard", None),
        P("rep", "shard", None),
        P("rep", "shard", None),
        P("rep", None, None),
        P("rep", None),
        P(),
    )
    return jax.shard_map(
        body,
        mesh=mesh,
        in_specs=placed,
        out_specs=(P("rep", "shard", None), P("rep", "shard", None), P("rep", "shard", None)),
        check_vma=False,
    )
```

```python
import jax
import jax.numpy as jnp
from jax import lax
from jax.experimental import pallas as pl
from jax.experimental.pallas import tpu as pltpu
from jax.sharding import PartitionSpec as P


HEADS = 16
HEAD_DIM = 64
TILE = 128
KB = 6


momentum_beta = 0.9


def partner(value, axis, bit):
    return lax.ppermute(value, axis, [(i, i ^ 1 << bit) for i in range(lax.axis_size(axis))])


def add_rows(source, shard_rows):
    return jnp.dot(source, shard_rows, preferred_element_type=jnp.float32)


def attention_kernel(index_ref, live_ref, query_ref, *refs):
    kv_refs = refs[:KB]
    out_ref = refs[KB]
    tile = pl.program_id(0)
    live = live_ref[tile]
    model_width = query_ref.shape[1]
    pair_width = 2 * HEAD_DIM
    lane = lax.broadcasted_iota(jnp.int32, (TILE, pair_width), 1)
    first_half = lane < HEAD_DIM
    slot_of = lax.broadcasted_iota(jnp.int32, (TILE, KB * TILE), 1) // TILE
    usable = slot_of < live
    for pair in range(HEADS // 2):
        lo = pair * pair_width
        query_pair = query_ref[:, lo:lo + pair_width]
        keys = [kv_refs[j][0, :, lo:lo + pair_width] for j in range(KB)]
        values = [kv_refs[j][0, :, model_width + lo:model_width + lo + pair_width] for j in range(KB)]
        outs = []
        for half in range(2):
            keep = first_half if half == 0 else jnp.logical_not(first_half)
            query_head = jnp.where(keep, query_pair, jnp.zeros_like(query_pair))
            scores = jnp.concatenate(
                [
                    lax.dot_general(
                        query_head, keys[j], (((1,), (1,)), ((), ())),
                        preferred_element_type=jnp.float32,
                    )
                    for j in range(KB)
                ],
                axis=1,
            ) * jnp.float32(HEAD_DIM ** (-0.5))
            scores = jnp.where(usable, scores, jnp.float32(-1e30))
            row_max = jnp.max(scores, axis=1, keepdims=True)
            exponent = jnp.exp(scores - row_max)
            inverse = 1.0 / jnp.sum(exponent, axis=1, keepdims=True)
            weights = exponent.astype(jnp.bfloat16)
            mixture = jnp.zeros((TILE, pair_width), jnp.float32)
            for j in range(KB):
                mixture = mixture + jnp.dot(
                    weights[:, j * TILE:(j + 1) * TILE], values[j],
                    preferred_element_type=jnp.float32,
                )
            mixture = mixture * inverse
            outs.append(mixture)
        joined = jnp.where(first_half, outs[0], outs[1])
        out_ref[:, lo:lo + pair_width] = joined.astype(out_ref.dtype)


def attend(query, kv_table, slot_index, live_mine):
    row_count, model_width = query.shape
    tile_count = row_count // TILE

    def kv_spec(j):
        return pl.BlockSpec(
            (1, TILE, 2 * model_width), lambda t, idx, live: (idx[t * KB + j], 0, 0)
        )

    grid_spec = pltpu.PrefetchScalarGridSpec(
        num_scalar_prefetch=2,
        grid=(tile_count,),
        in_specs=[pl.BlockSpec((TILE, model_width), lambda t, idx, live: (t, 0))]
        + [kv_spec(j) for j in range(KB)],
        out_specs=pl.BlockSpec((TILE, model_width), lambda t, idx, live: (t, 0)),
    )
    return pl.pallas_call(
        attention_kernel,
        grid_spec=grid_spec,
        out_shape=jax.ShapeDtypeStruct((row_count, model_width), jnp.bfloat16),
        compiler_params=pltpu.CompilerParams(dimension_semantics=("arbitrary",)),
    )(slot_index, live_mine, query, *([kv_table] * KB))


def pick_partner(bit_choice, bit_count, value):
    candidates = [partner(value, "rep", bit_number) for bit_number in range(bit_count)]
    return jax.tree.map(
        lambda *parts: lax.select_n(bit_choice, *parts) if len(parts) > 1 else parts[0],
        *candidates,
    )


def body(
    cell_features, upstream, qkv_weight, out_weight, momentum, key_tiles, live_blocks, step_index
):
    features = cell_features[0]
    row_count, model_width = features.shape
    tile_count = row_count // TILE
    shard_count = lax.axis_size("shard")
    my_index = lax.axis_index("shard")
    slot_count = tile_count * KB
    remote_count = slot_count - slot_count // 2
    capacity = (remote_count + shard_count - 2) // (shard_count - 1)
    requests = key_tiles[0].reshape(shard_count, slot_count)
    owners = requests // tile_count
    local_tile = requests % tile_count
    positions = jnp.arange(slot_count, dtype=jnp.int32)
    earlier = positions[None, :] < positions[:, None]
    same_owner = owners[:, :, None] == owners[:, None, :]
    owner_rank = jnp.sum((same_owner & earlier[None]).astype(jnp.int32), axis=2)
    offsets = jnp.arange(1, shard_count, dtype=jnp.int32)
    receivers = (my_index + offsets) % shard_count
    their_owners = owners[receivers]
    their_ranks = owner_rank[receivers]
    their_local = local_tile[receivers]
    slot_ids = jnp.arange(capacity, dtype=jnp.int32)
    chosen = ((their_owners == my_index)[:, :, None]) & (their_ranks[:, :, None] == slot_ids[None, None, :])
    send_index = jnp.sum(chosen.astype(jnp.int32) * their_local[:, :, None], axis=1)
    feature_tiles = features.reshape(tile_count, TILE, model_width)
    outgoing = feature_tiles[send_index.reshape(-1)].reshape(
        shard_count - 1, capacity, TILE, model_width
    )
    arrived = [
        lax.ppermute(
            outgoing[k - 1],
            "shard",
            [(i, (i + k) % shard_count) for i in range(shard_count)],
        )
        for k in range(1, shard_count)
    ]
    arrived_rows = jnp.concatenate(arrived, axis=0).reshape(-1, model_width)
    bit_count = lax.axis_size("rep").bit_length() - 1
    bit_choice = step_index % bit_count
    own_weight = out_weight[0]
    own_moment = momentum[0]
    their_weight, their_moment = pick_partner(bit_choice, bit_count, (own_weight, own_moment))
    arrived_rows, their_weight, their_moment = lax.optimization_barrier(
        (arrived_rows, their_weight, their_moment)
    )
    my_owners = lax.dynamic_index_in_dim(owners, my_index, 0, keepdims=False)
    my_ranks = lax.dynamic_index_in_dim(owner_rank, my_index, 0, keepdims=False)
    my_local = lax.dynamic_index_in_dim(local_tile, my_index, 0, keepdims=False)
    my_remote = my_owners != my_index
    my_offset = (my_index - my_owners) % shard_count
    table_size = tile_count + (shard_count - 1) * capacity
    slot_index = jnp.where(my_remote, tile_count + (my_offset - 1) * capacity + my_ranks, my_local)
    slot_index = jnp.clip(slot_index, 0, table_size - 1).astype(jnp.int32)
    kv_weight = lax.all_gather(qkv_weight[0][:, model_width:], "shard", axis=0, tiled=True)
    kv_table = add_rows(
        jnp.concatenate([features, arrived_rows], axis=0), kv_weight
    ).astype(jnp.bfloat16).reshape(table_size, TILE, 2 * model_width)
    query_weight = lax.all_gather(qkv_weight[0][:, :model_width], "shard", axis=0, tiled=True)
    query = add_rows(features, query_weight).astype(jnp.bfloat16)
    live_mine = lax.dynamic_slice_in_dim(live_blocks[0], my_index * tile_count, tile_count, 0)
    attended = attend(query, kv_table, slot_index, live_mine.astype(jnp.int32))
    product = add_rows(attended, lax.all_gather(out_weight[0], "shard", axis=0, tiled=True))
    layer_out = (features.astype(jnp.float32) + product).astype(jnp.bfloat16)
    partial = lax.dot_general(
        attended, upstream[0], (((0,), (0,)), ((), ())), preferred_element_type=jnp.float32
    ).astype(jnp.bfloat16)
    block_rows = partial.shape[0] // shard_count
    blocks = partial.reshape(shard_count, block_rows, partial.shape[1])
    gradient = lax.dynamic_index_in_dim(blocks, my_index, 0, keepdims=False).astype(jnp.float32)
    for k in range(1, shard_count):
        piece = lax.dynamic_index_in_dim(blocks, (my_index + k) % shard_count, 0, keepdims=False)
        received = lax.ppermute(
            piece, "shard", [(i, (i + k) % shard_count) for i in range(shard_count)]
        )
        if k == 1:
            received, layer_out = lax.optimization_barrier((received, layer_out))
        gradient = gradient + received.astype(jnp.float32)
    learn_rate = jnp.float32(50.0) / (jnp.float32(500.0) + step_index.astype(jnp.float32))
    their_gradient = pick_partner(bit_choice, bit_count, gradient.astype(jnp.bfloat16))
    velocity = momentum_beta * own_moment + gradient
    their_velocity = momentum_beta * their_moment + their_gradient.astype(jnp.float32)
    stepped = (own_weight.astype(jnp.float32) - learn_rate * velocity).astype(jnp.bfloat16)
    their_stepped = (
        their_weight.astype(jnp.float32) - learn_rate * their_velocity
    ).astype(jnp.bfloat16)
    new_weight = (
        0.5 * (stepped.astype(jnp.float32) + their_stepped.astype(jnp.float32))
    ).astype(jnp.bfloat16)
    new_momentum = 0.5 * (velocity + their_velocity)
    return (layer_out[None], new_weight[None], new_momentum[None])


def solution(mesh):
    placed = (
        P("rep", "shard", None),
        P("rep", "shard", None),
        P("rep", "shard", None),
        P("rep", "shard", None),
        P("rep", "shard", None),
        P("rep", None, None),
        P("rep", None),
        P(),
    )

    return jax.shard_map(
        body,
        mesh=mesh,
        in_specs=placed,
        out_specs=(P("rep", "shard", None), P("rep", "shard", None), P("rep", "shard", None)),
        check_vma=False,
    )
```

```python
import functools

import jax
import jax.numpy as jnp
from jax import lax
from jax.experimental import pallas as pl
from jax.experimental.pallas import tpu as pltpu
from jax.sharding import PartitionSpec as P

HEADS = 16
HEAD_DIM = 64
TILE = 128
KB = 6


momentum_beta = 0.9


def shortened(value):

    def short(part):
        return part.astype(jnp.bfloat16) if part.dtype == jnp.float32 else part

    return jax.tree.map(short, value)


def partner(value, axis, bit):
    return lax.ppermute(value, axis, [(i, i ^ 1 << bit) for i in range(lax.axis_size(axis))])


def add_rows(source, shard_rows):
    return jnp.dot(source, shard_rows, preferred_element_type=jnp.float32)


def attention_kernel(index_ref, live_ref, query_ref, *refs):
    kv_refs = refs[:KB]
    out_ref = refs[KB]
    tile = pl.program_id(0)
    live = live_ref[tile]
    model_width = query_ref.shape[1]
    pair_width = 2 * HEAD_DIM
    lane = lax.broadcasted_iota(jnp.int32, (TILE, pair_width), 1)
    first_half = lane < HEAD_DIM

    def attend_pairs(used):

        def one_pair(pair, carry):
            lo = pl.multiple_of(pair * pair_width, pair_width)
            query_pair = query_ref[:, pl.ds(lo, pair_width)]
            keys = [kv_refs[j][0, :, pl.ds(lo, pair_width)] for j in range(used)]
            values = [
                kv_refs[j][0, :, pl.ds(model_width + lo, pair_width)] for j in range(used)
            ]
            outs = []
            for half in range(2):
                keep = first_half if half == 0 else jnp.logical_not(first_half)
                query_head = jnp.where(keep, query_pair, jnp.zeros_like(query_pair))
                parts = [
                    lax.dot_general(
                        query_head, keys[j], (((1,), (1,)), ((), ())),
                        preferred_element_type=jnp.float32,
                    )
                    for j in range(used)
                ]
                scores = (parts[0] if used == 1 else jnp.concatenate(parts, axis=1)) * jnp.float32(
                    HEAD_DIM ** (-0.5)
                )
                row_max = jnp.max(scores, axis=1, keepdims=True)
                exponent = jnp.exp(scores - row_max)
                inverse = 1.0 / jnp.sum(exponent, axis=1, keepdims=True)
                weights = exponent.astype(jnp.bfloat16)
                mixture = jnp.zeros((TILE, pair_width), jnp.float32)
                for j in range(used):
                    mixture = mixture + jnp.dot(
                        weights[:, j * TILE:(j + 1) * TILE], values[j],
                        preferred_element_type=jnp.float32,
                    )
                outs.append(mixture * inverse)
            joined = jnp.where(first_half, outs[0], outs[1])
            out_ref[:, pl.ds(lo, pair_width)] = joined.astype(out_ref.dtype)
            return carry

        lax.fori_loop(0, HEADS // 2, one_pair, 0)

    for used in range(1, KB + 1):
        pl.when(live == used)(functools.partial(attend_pairs, used))


def attend(query, kv_table, slot_index, live_mine):
    row_count, model_width = query.shape
    tile_count = row_count // TILE

    def kv_spec(j):
        return pl.BlockSpec(
            (1, TILE, 2 * model_width), lambda t, idx, live: (idx[t * KB + j], 0, 0)
        )

    grid_spec = pltpu.PrefetchScalarGridSpec(
        num_scalar_prefetch=2,
        grid=(tile_count,),
        in_specs=[pl.BlockSpec((TILE, model_width), lambda t, idx, live: (t, 0))]
        + [kv_spec(j) for j in range(KB)],
        out_specs=pl.BlockSpec((TILE, model_width), lambda t, idx, live: (t, 0)),
    )
    return pl.pallas_call(
        attention_kernel,
        grid_spec=grid_spec,
        out_shape=jax.ShapeDtypeStruct((row_count, model_width), jnp.bfloat16),
        compiler_params=pltpu.CompilerParams(dimension_semantics=("arbitrary",)),
    )(slot_index, live_mine, query, *([kv_table] * KB))


def pick_partner(bit_choice, bit_count, value):
    candidates = [partner(value, "rep", bit_number) for bit_number in range(bit_count)]
    return jax.tree.map(
        lambda *parts: lax.select_n(bit_choice, *parts) if len(parts) > 1 else parts[0],
        *candidates,
    )


def body(
    cell_features, upstream, qkv_weight, out_weight, momentum, key_tiles, live_blocks, step_index
):
    features = cell_features[0]
    row_count, model_width = features.shape
    tile_count = row_count // TILE
    shard_count = lax.axis_size("shard")
    my_index = lax.axis_index("shard")
    slot_count = tile_count * KB
    remote_count = slot_count - slot_count // 2
    capacity = (remote_count + shard_count - 2) // (shard_count - 1)
    requests = key_tiles[0].reshape(shard_count, slot_count)
    owners = requests // tile_count
    local_tile = requests % tile_count
    positions = jnp.arange(slot_count, dtype=jnp.int32)
    earlier = positions[None, :] < positions[:, None]
    same_owner = owners[:, :, None] == owners[:, None, :]
    owner_rank = jnp.sum((same_owner & earlier[None]).astype(jnp.int32), axis=2)
    offsets = jnp.arange(1, shard_count, dtype=jnp.int32)
    receivers = (my_index + offsets) % shard_count
    their_owners = owners[receivers]
    their_ranks = owner_rank[receivers]
    their_local = local_tile[receivers]
    slot_ids = jnp.arange(capacity, dtype=jnp.int32)
    chosen = ((their_owners == my_index)[:, :, None]) & (their_ranks[:, :, None] == slot_ids[None, None, :])
    send_index = jnp.sum(chosen.astype(jnp.int32) * their_local[:, :, None], axis=1)
    feature_tiles = features.reshape(tile_count, TILE, model_width)
    outgoing = feature_tiles[send_index.reshape(-1)].reshape(
        shard_count - 1, capacity, TILE, model_width
    )
    arrived = [
        lax.ppermute(
            outgoing[k - 1],
            "shard",
            [(i, (i + k) % shard_count) for i in range(shard_count)],
        )
        for k in range(1, shard_count)
    ]
    arrived_rows = jnp.concatenate(arrived, axis=0).reshape(-1, model_width)
    bit_count = lax.axis_size("rep").bit_length() - 1
    bit_choice = step_index % bit_count
    own_weight = out_weight[0]
    own_moment = momentum[0]
    their_weight, their_moment = pick_partner(bit_choice, bit_count, (own_weight, own_moment))
    arrived_rows, their_weight, their_moment = lax.optimization_barrier(
        (arrived_rows, their_weight, their_moment)
    )
    my_owners = lax.dynamic_index_in_dim(owners, my_index, 0, keepdims=False)
    my_ranks = lax.dynamic_index_in_dim(owner_rank, my_index, 0, keepdims=False)
    my_local = lax.dynamic_index_in_dim(local_tile, my_index, 0, keepdims=False)
    my_remote = my_owners != my_index
    my_offset = (my_index - my_owners) % shard_count
    table_size = tile_count + (shard_count - 1) * capacity
    slot_index = jnp.where(my_remote, tile_count + (my_offset - 1) * capacity + my_ranks, my_local)
    slot_index = jnp.clip(slot_index, 0, table_size - 1).astype(jnp.int32)
    full_qkv = lax.all_gather(qkv_weight[0], "shard", axis=0, tiled=True)
    query = add_rows(features, full_qkv[:, :model_width]).astype(jnp.bfloat16)
    kv_table = add_rows(
        jnp.concatenate([features, arrived_rows], axis=0), full_qkv[:, model_width:]
    ).astype(jnp.bfloat16).reshape(table_size, TILE, 2 * model_width)
    live_mine = lax.dynamic_slice_in_dim(live_blocks[0], my_index * tile_count, tile_count, 0)
    live_mine = jnp.clip(live_mine, 1, KB).astype(jnp.int32)
    attended = attend(query, kv_table, slot_index, live_mine)
    product = add_rows(attended, lax.all_gather(out_weight[0], "shard", axis=0, tiled=True))
    layer_out = (features.astype(jnp.float32) + product).astype(jnp.bfloat16)
    partial = lax.dot_general(
        attended, upstream[0], (((0,), (0,)), ((), ())), preferred_element_type=jnp.float32
    ).astype(jnp.bfloat16)
    block_rows = partial.shape[0] // shard_count
    blocks = partial.reshape(shard_count, block_rows, partial.shape[1])
    gradient = lax.dynamic_index_in_dim(blocks, my_index, 0, keepdims=False).astype(jnp.float32)
    for k in range(1, shard_count):
        piece = lax.dynamic_index_in_dim(blocks, (my_index + k) % shard_count, 0, keepdims=False)
        received = lax.ppermute(
            piece, "shard", [(i, (i + k) % shard_count) for i in range(shard_count)]
        )
        if k == 1:
            received, layer_out = lax.optimization_barrier((received, layer_out))
        gradient = gradient + received.astype(jnp.float32)
    learn_rate = jnp.float32(50.0) / (jnp.float32(500.0) + step_index.astype(jnp.float32))
    their_gradient = pick_partner(bit_choice, bit_count, gradient.astype(jnp.bfloat16))
    velocity = momentum_beta * own_moment + gradient
    their_velocity = momentum_beta * their_moment + their_gradient.astype(jnp.float32)
    stepped = (own_weight.astype(jnp.float32) - learn_rate * velocity).astype(jnp.bfloat16)
    their_stepped = (
        their_weight.astype(jnp.float32) - learn_rate * their_velocity
    ).astype(jnp.bfloat16)
    new_weight = (
        0.5 * (stepped.astype(jnp.float32) + their_stepped.astype(jnp.float32))
    ).astype(jnp.bfloat16)
    new_momentum = 0.5 * (velocity + their_velocity)
    return (layer_out[None], new_weight[None], new_momentum[None])


def solution(mesh):
    placed = (
        P("rep", "shard", None),
        P("rep", "shard", None),
        P("rep", "shard", None),
        P("rep", "shard", None),
        P("rep", "shard", None),
        P("rep", None, None),
        P("rep", None),
        P(),
    )
    return jax.shard_map(
        body,
        mesh=mesh,
        in_specs=placed,
        out_specs=(P("rep", "shard", None), P("rep", "shard", None), P("rep", "shard", None)),
        check_vma=False,
    )
```

```python
import functools

import jax
import jax.numpy as jnp
from jax import lax
from jax.experimental import pallas as pl
from jax.experimental.pallas import tpu as pltpu
from jax.sharding import PartitionSpec as P

HEADS = 16
HEAD_DIM = 64
TILE = 128
KB = 6


momentum_beta = 0.9


def shortened(value):

    def short(part):
        return part.astype(jnp.bfloat16) if part.dtype == jnp.float32 else part

    return jax.tree.map(short, value)


def partner(value, axis, bit):
    return lax.ppermute(value, axis, [(i, i ^ 1 << bit) for i in range(lax.axis_size(axis))])


def add_rows(source, shard_rows):
    return jnp.dot(source, shard_rows, preferred_element_type=jnp.float32)


def attention_kernel(index_ref, live_ref, query_ref, *refs):
    kv_refs = refs[:KB]
    out_ref = refs[KB]
    tile = pl.program_id(0)
    live = live_ref[tile]
    model_width = query_ref.shape[1]
    pair_width = 2 * HEAD_DIM
    lane = lax.broadcasted_iota(jnp.int32, (TILE, pair_width), 1)
    first_half = lane < HEAD_DIM

    def attend_pairs(used):

        def one_pair(pair, carry):
            lo = pl.multiple_of(pair * pair_width, pair_width)
            query_pair = query_ref[:, pl.ds(lo, pair_width)]
            keys = [kv_refs[j][0, :, pl.ds(lo, pair_width)] for j in range(used)]
            values = [
                kv_refs[j][0, :, pl.ds(model_width + lo, pair_width)] for j in range(used)
            ]
            outs = []
            for half in range(2):
                keep = first_half if half == 0 else jnp.logical_not(first_half)
                query_head = jnp.where(keep, query_pair, jnp.zeros_like(query_pair))
                parts = [
                    lax.dot_general(
                        query_head, keys[j], (((1,), (1,)), ((), ())),
                        preferred_element_type=jnp.float32,
                    )
                    for j in range(used)
                ]
                scores = (parts[0] if used == 1 else jnp.concatenate(parts, axis=1)) * jnp.float32(
                    HEAD_DIM ** (-0.5)
                )
                row_max = jnp.max(scores, axis=1, keepdims=True)
                exponent = jnp.exp(scores - row_max)
                inverse = 1.0 / jnp.sum(exponent, axis=1, keepdims=True)
                weights = exponent.astype(jnp.bfloat16)
                mixture = jnp.zeros((TILE, pair_width), jnp.float32)
                for j in range(used):
                    mixture = mixture + jnp.dot(
                        weights[:, j * TILE:(j + 1) * TILE], values[j],
                        preferred_element_type=jnp.float32,
                    )
                outs.append(mixture * inverse)
            joined = jnp.where(first_half, outs[0], outs[1])
            out_ref[:, pl.ds(lo, pair_width)] = joined.astype(out_ref.dtype)
            return carry

        lax.fori_loop(0, HEADS // 2, one_pair, 0)

    for used in range(1, KB + 1):
        pl.when(live == used)(functools.partial(attend_pairs, used))


def attend(query, kv_table, slot_index, live_mine):
    row_count, model_width = query.shape
    tile_count = row_count // TILE

    def kv_spec(j):
        return pl.BlockSpec(
            (1, TILE, 2 * model_width), lambda t, idx, live: (idx[t * KB + j], 0, 0)
        )

    grid_spec = pltpu.PrefetchScalarGridSpec(
        num_scalar_prefetch=2,
        grid=(tile_count,),
        in_specs=[pl.BlockSpec((TILE, model_width), lambda t, idx, live: (t, 0))]
        + [kv_spec(j) for j in range(KB)],
        out_specs=pl.BlockSpec((TILE, model_width), lambda t, idx, live: (t, 0)),
    )
    return pl.pallas_call(
        attention_kernel,
        grid_spec=grid_spec,
        out_shape=jax.ShapeDtypeStruct((row_count, model_width), jnp.bfloat16),
        compiler_params=pltpu.CompilerParams(dimension_semantics=("arbitrary",)),
    )(slot_index, live_mine, query, *([kv_table] * KB))


def pick_partner(bit_choice, bit_count, value):
    candidates = [partner(value, "rep", bit_number) for bit_number in range(bit_count)]
    return jax.tree.map(
        lambda *parts: lax.select_n(bit_choice, *parts) if len(parts) > 1 else parts[0],
        *candidates,
    )


def body(
    cell_features, upstream, qkv_weight, out_weight, momentum, key_tiles, live_blocks, step_index
):
    features = cell_features[0]
    row_count, model_width = features.shape
    tile_count = row_count // TILE
    shard_count = lax.axis_size("shard")
    my_index = lax.axis_index("shard")
    slot_count = tile_count * KB
    remote_count = slot_count - slot_count // 2
    capacity = (remote_count + shard_count - 2) // (shard_count - 1)
    requests = key_tiles[0].reshape(shard_count, slot_count)
    owners = requests // tile_count
    local_tile = requests % tile_count
    positions = jnp.arange(slot_count, dtype=jnp.int32)
    earlier = positions[None, :] < positions[:, None]
    same_owner = owners[:, :, None] == owners[:, None, :]
    owner_rank = jnp.sum((same_owner & earlier[None]).astype(jnp.int32), axis=2)
    offsets = jnp.arange(1, shard_count, dtype=jnp.int32)
    receivers = (my_index + offsets) % shard_count
    their_owners = owners[receivers]
    their_ranks = owner_rank[receivers]
    their_local = local_tile[receivers]
    slot_ids = jnp.arange(capacity, dtype=jnp.int32)
    chosen = ((their_owners == my_index)[:, :, None]) & (their_ranks[:, :, None] == slot_ids[None, None, :])
    send_index = jnp.sum(chosen.astype(jnp.int32) * their_local[:, :, None], axis=1)
    feature_tiles = features.reshape(tile_count, TILE, model_width)
    outgoing = feature_tiles[send_index.reshape(-1)].reshape(
        shard_count - 1, capacity, TILE, model_width
    )
    full_qkv = lax.all_gather(qkv_weight[0], "shard", axis=0, tiled=True)
    outgoing, full_qkv = lax.optimization_barrier((outgoing, full_qkv))
    arrived = [
        lax.ppermute(
            outgoing[k - 1],
            "shard",
            [(i, (i + k) % shard_count) for i in range(shard_count)],
        )
        for k in range(1, shard_count)
    ]
    arrived_rows = jnp.concatenate(arrived, axis=0).reshape(-1, model_width)
    bit_count = lax.axis_size("rep").bit_length() - 1
    bit_choice = step_index % bit_count
    own_weight = out_weight[0]
    own_moment = momentum[0]
    their_weight, their_moment = pick_partner(bit_choice, bit_count, (own_weight, own_moment))
    arrived_rows, their_weight, their_moment = lax.optimization_barrier(
        (arrived_rows, their_weight, their_moment)
    )
    my_owners = lax.dynamic_index_in_dim(owners, my_index, 0, keepdims=False)
    my_ranks = lax.dynamic_index_in_dim(owner_rank, my_index, 0, keepdims=False)
    my_local = lax.dynamic_index_in_dim(local_tile, my_index, 0, keepdims=False)
    my_remote = my_owners != my_index
    my_offset = (my_index - my_owners) % shard_count
    table_size = tile_count + (shard_count - 1) * capacity
    slot_index = jnp.where(my_remote, tile_count + (my_offset - 1) * capacity + my_ranks, my_local)
    slot_index = jnp.clip(slot_index, 0, table_size - 1).astype(jnp.int32)
    query = add_rows(features, full_qkv[:, :model_width]).astype(jnp.bfloat16)
    local_kv = add_rows(features, full_qkv[:, model_width:]).astype(jnp.bfloat16)
    query, local_kv, arrived_rows = lax.optimization_barrier((query, local_kv, arrived_rows))
    remote_kv = add_rows(arrived_rows, full_qkv[:, model_width:]).astype(jnp.bfloat16)
    kv_table = jnp.concatenate([local_kv, remote_kv], axis=0).reshape(
        table_size, TILE, 2 * model_width
    )
    live_mine = lax.dynamic_slice_in_dim(live_blocks[0], my_index * tile_count, tile_count, 0)
    live_mine = jnp.clip(live_mine, 1, KB).astype(jnp.int32)
    attended = attend(query, kv_table, slot_index, live_mine)
    product = add_rows(attended, lax.all_gather(out_weight[0], "shard", axis=0, tiled=True))
    layer_out = (features.astype(jnp.float32) + product).astype(jnp.bfloat16)
    partial = lax.dot_general(
        attended, upstream[0], (((0,), (0,)), ((), ())), preferred_element_type=jnp.float32
    ).astype(jnp.bfloat16)
    block_rows = partial.shape[0] // shard_count
    blocks = partial.reshape(shard_count, block_rows, partial.shape[1])
    gradient = lax.dynamic_index_in_dim(blocks, my_index, 0, keepdims=False).astype(jnp.float32)
    for k in range(1, shard_count):
        piece = lax.dynamic_index_in_dim(blocks, (my_index + k) % shard_count, 0, keepdims=False)
        received = lax.ppermute(
            piece, "shard", [(i, (i + k) % shard_count) for i in range(shard_count)]
        )
        if k == 1:
            received, layer_out = lax.optimization_barrier((received, layer_out))
        gradient = gradient + received.astype(jnp.float32)
    learn_rate = jnp.float32(50.0) / (jnp.float32(500.0) + step_index.astype(jnp.float32))
    their_gradient = pick_partner(bit_choice, bit_count, gradient.astype(jnp.bfloat16))
    velocity = momentum_beta * own_moment + gradient
    their_velocity = momentum_beta * their_moment + their_gradient.astype(jnp.float32)
    stepped = (own_weight.astype(jnp.float32) - learn_rate * velocity).astype(jnp.bfloat16)
    their_stepped = (
        their_weight.astype(jnp.float32) - learn_rate * their_velocity
    ).astype(jnp.bfloat16)
    new_weight = (
        0.5 * (stepped.astype(jnp.float32) + their_stepped.astype(jnp.float32))
    ).astype(jnp.bfloat16)
    new_momentum = 0.5 * (velocity + their_velocity)
    return (layer_out[None], new_weight[None], new_momentum[None])


def solution(mesh):
    placed = (
        P("rep", "shard", None),
        P("rep", "shard", None),
        P("rep", "shard", None),
        P("rep", "shard", None),
        P("rep", "shard", None),
        P("rep", None, None),
        P("rep", None),
        P(),
    )
    return jax.shard_map(
        body,
        mesh=mesh,
        in_specs=placed,
        out_specs=(P("rep", "shard", None), P("rep", "shard", None), P("rep", "shard", None)),
        check_vma=False,
    )
```

```python
import functools

import jax
import jax.numpy as jnp
from jax import lax
from jax.experimental import pallas as pl
from jax.experimental.pallas import tpu as pltpu
from jax.sharding import PartitionSpec as P

HEADS = 16
HEAD_DIM = 64
TILE = 128
KB = 6


momentum_beta = 0.9


def shortened(value):

    def short(part):
        return part.astype(jnp.bfloat16) if part.dtype == jnp.float32 else part

    return jax.tree.map(short, value)


def partner(value, axis, bit):
    return lax.ppermute(value, axis, [(i, i ^ 1 << bit) for i in range(lax.axis_size(axis))])


def add_rows(source, shard_rows):
    return jnp.dot(source, shard_rows, preferred_element_type=jnp.float32)


def attention_kernel(index_ref, live_ref, query_ref, *refs):
    kv_refs = refs[:KB]
    out_ref = refs[KB]
    tile = pl.program_id(0)
    live = live_ref[tile]
    model_width = query_ref.shape[1]
    slot_of = lax.broadcasted_iota(jnp.int32, (TILE, KB * TILE), 1) // TILE
    usable = slot_of < live
    for head in range(HEADS):
        lo = head * HEAD_DIM
        query_head = query_ref[:, lo:lo + HEAD_DIM]
        scores = jnp.concatenate(
            [
                lax.dot_general(
                    query_head, kv_refs[j][0, :, lo:lo + HEAD_DIM], (((1,), (1,)), ((), ())),
                    preferred_element_type=jnp.float32,
                )
                for j in range(KB)
            ],
            axis=1,
        ) * jnp.float32(HEAD_DIM ** (-0.5))
        scores = jnp.where(usable, scores, jnp.float32(-1e30))
        row_max = jnp.max(scores, axis=1, keepdims=True)
        exponent = jnp.exp(scores - row_max)
        inverse = 1.0 / jnp.sum(exponent, axis=1, keepdims=True)
        weights = exponent.astype(jnp.bfloat16)
        mixture = jnp.zeros((TILE, HEAD_DIM), jnp.float32)
        for j in range(KB):
            mixture = mixture + jnp.dot(
                weights[:, j * TILE:(j + 1) * TILE],
                kv_refs[j][0, :, model_width + lo:model_width + lo + HEAD_DIM],
                preferred_element_type=jnp.float32,
            )
        out_ref[:, lo:lo + HEAD_DIM] = (mixture * inverse).astype(out_ref.dtype)


def attend(query, kv_table, slot_index, live_mine):
    row_count, model_width = query.shape
    tile_count = row_count // TILE

    def kv_spec(j):
        return pl.BlockSpec(
            (1, TILE, 2 * model_width), lambda t, idx, live: (idx[t * KB + j], 0, 0)
        )

    grid_spec = pltpu.PrefetchScalarGridSpec(
        num_scalar_prefetch=2,
        grid=(tile_count,),
        in_specs=[pl.BlockSpec((TILE, model_width), lambda t, idx, live: (t, 0))]
        + [kv_spec(j) for j in range(KB)],
        out_specs=pl.BlockSpec((TILE, model_width), lambda t, idx, live: (t, 0)),
    )
    return pl.pallas_call(
        attention_kernel,
        grid_spec=grid_spec,
        out_shape=jax.ShapeDtypeStruct((row_count, model_width), jnp.bfloat16),
        compiler_params=pltpu.CompilerParams(dimension_semantics=("arbitrary",)),
    )(slot_index, live_mine, query, *([kv_table] * KB))


def pick_partner(bit_choice, bit_count, value):
    candidates = [partner(value, "rep", bit_number) for bit_number in range(bit_count)]
    return jax.tree.map(
        lambda *parts: lax.select_n(bit_choice, *parts) if len(parts) > 1 else parts[0],
        *candidates,
    )


def body(
    cell_features, upstream, qkv_weight, out_weight, momentum, key_tiles, live_blocks, step_index
):
    features = cell_features[0]
    row_count, model_width = features.shape
    tile_count = row_count // TILE
    shard_count = lax.axis_size("shard")
    my_index = lax.axis_index("shard")
    slot_count = tile_count * KB
    remote_count = slot_count - slot_count // 2
    capacity = (remote_count + shard_count - 2) // (shard_count - 1)
    requests = key_tiles[0].reshape(shard_count, slot_count)
    owners = requests // tile_count
    local_tile = requests % tile_count
    positions = jnp.arange(slot_count, dtype=jnp.int32)
    earlier = positions[None, :] < positions[:, None]
    same_owner = owners[:, :, None] == owners[:, None, :]
    owner_rank = jnp.sum((same_owner & earlier[None]).astype(jnp.int32), axis=2)
    offsets = jnp.arange(1, shard_count, dtype=jnp.int32)
    receivers = (my_index + offsets) % shard_count
    their_owners = owners[receivers]
    their_ranks = owner_rank[receivers]
    their_local = local_tile[receivers]
    slot_ids = jnp.arange(capacity, dtype=jnp.int32)
    chosen = ((their_owners == my_index)[:, :, None]) & (their_ranks[:, :, None] == slot_ids[None, None, :])
    send_index = jnp.sum(chosen.astype(jnp.int32) * their_local[:, :, None], axis=1)
    feature_tiles = features.reshape(tile_count, TILE, model_width)
    outgoing = feature_tiles[send_index.reshape(-1)].reshape(
        shard_count - 1, capacity, TILE, model_width
    )
    arrived = [
        lax.ppermute(
            outgoing[k - 1],
            "shard",
            [(i, (i + k) % shard_count) for i in range(shard_count)],
        )
        for k in range(1, shard_count)
    ]
    arrived_rows = jnp.concatenate(arrived, axis=0).reshape(-1, model_width)
    bit_count = lax.axis_size("rep").bit_length() - 1
    bit_choice = step_index % bit_count
    own_weight = out_weight[0]
    own_moment = momentum[0]
    their_weight, their_moment = pick_partner(bit_choice, bit_count, (own_weight, own_moment))
    arrived_rows, their_weight, their_moment = lax.optimization_barrier(
        (arrived_rows, their_weight, their_moment)
    )
    my_owners = lax.dynamic_index_in_dim(owners, my_index, 0, keepdims=False)
    my_ranks = lax.dynamic_index_in_dim(owner_rank, my_index, 0, keepdims=False)
    my_local = lax.dynamic_index_in_dim(local_tile, my_index, 0, keepdims=False)
    my_remote = my_owners != my_index
    my_offset = (my_index - my_owners) % shard_count
    table_size = tile_count + (shard_count - 1) * capacity
    slot_index = jnp.where(my_remote, tile_count + (my_offset - 1) * capacity + my_ranks, my_local)
    slot_index = jnp.clip(slot_index, 0, table_size - 1).astype(jnp.int32)
    full_qkv = lax.all_gather(qkv_weight[0], "shard", axis=0, tiled=True)
    query = add_rows(features, full_qkv[:, :model_width]).astype(jnp.bfloat16)
    kv_table = add_rows(
        jnp.concatenate([features, arrived_rows], axis=0), full_qkv[:, model_width:]
    ).astype(jnp.bfloat16).reshape(table_size, TILE, 2 * model_width)
    live_mine = lax.dynamic_slice_in_dim(live_blocks[0], my_index * tile_count, tile_count, 0)
    attended = attend(query, kv_table, slot_index, live_mine.astype(jnp.int32))
    product = add_rows(attended, lax.all_gather(out_weight[0], "shard", axis=0, tiled=True))
    layer_out = (features.astype(jnp.float32) + product).astype(jnp.bfloat16)
    partial = lax.dot_general(
        attended, upstream[0], (((0,), (0,)), ((), ())), preferred_element_type=jnp.float32
    ).astype(jnp.bfloat16)
    block_rows = partial.shape[0] // shard_count
    blocks = partial.reshape(shard_count, block_rows, partial.shape[1])
    gradient = lax.dynamic_index_in_dim(blocks, my_index, 0, keepdims=False).astype(jnp.float32)
    for k in range(1, shard_count):
        piece = lax.dynamic_index_in_dim(blocks, (my_index + k) % shard_count, 0, keepdims=False)
        received = lax.ppermute(
            piece, "shard", [(i, (i + k) % shard_count) for i in range(shard_count)]
        )
        if k == 1:
            received, layer_out = lax.optimization_barrier((received, layer_out))
        gradient = gradient + received.astype(jnp.float32)
    learn_rate = jnp.float32(50.0) / (jnp.float32(500.0) + step_index.astype(jnp.float32))
    their_gradient = pick_partner(bit_choice, bit_count, gradient.astype(jnp.bfloat16))
    velocity = momentum_beta * own_moment + gradient
    their_velocity = momentum_beta * their_moment + their_gradient.astype(jnp.float32)
    stepped = (own_weight.astype(jnp.float32) - learn_rate * velocity).astype(jnp.bfloat16)
    their_stepped = (
        their_weight.astype(jnp.float32) - learn_rate * their_velocity
    ).astype(jnp.bfloat16)
    new_weight = (
        0.5 * (stepped.astype(jnp.float32) + their_stepped.astype(jnp.float32))
    ).astype(jnp.bfloat16)
    new_momentum = 0.5 * (velocity + their_velocity)
    return (layer_out[None], new_weight[None], new_momentum[None])


def solution(mesh):
    placed = (
        P("rep", "shard", None),
        P("rep", "shard", None),
        P("rep", "shard", None),
        P("rep", "shard", None),
        P("rep", "shard", None),
        P("rep", None, None),
        P("rep", None),
        P(),
    )
    return jax.shard_map(
        body,
        mesh=mesh,
        in_specs=placed,
        out_specs=(P("rep", "shard", None), P("rep", "shard", None), P("rep", "shard", None)),
        check_vma=False,
    )
```

```python
import functools

import jax
import jax.numpy as jnp
from jax import lax
from jax.experimental import pallas as pl
from jax.experimental.pallas import tpu as pltpu
from jax.sharding import PartitionSpec as P

HEADS = 16
HEAD_DIM = 64
TILE = 128
KB = 6


momentum_beta = 0.9


def shortened(value):

    def short(part):
        return part.astype(jnp.bfloat16) if part.dtype == jnp.float32 else part

    return jax.tree.map(short, value)


def partner(value, axis, bit):
    return lax.ppermute(value, axis, [(i, i ^ 1 << bit) for i in range(lax.axis_size(axis))])


def add_rows(source, shard_rows):
    return jnp.dot(source, shard_rows, preferred_element_type=jnp.float32)


def attention_kernel(index_ref, live_ref, query_ref, *refs):
    kv_refs = refs[:KB]
    out_ref = refs[KB]
    tile = pl.program_id(0)
    live = live_ref[tile]
    model_width = query_ref.shape[1]
    pair_width = 2 * HEAD_DIM
    lane = lax.broadcasted_iota(jnp.int32, (TILE, pair_width), 1)
    first_half = lane < HEAD_DIM
    slot_of = lax.broadcasted_iota(jnp.int32, (TILE, KB * TILE), 1) // TILE
    usable = slot_of < live
    for pair in range(HEADS // 2):
        lo = pair * pair_width
        query_pair = query_ref[:, lo:lo + pair_width]
        keys = [kv_refs[j][0, :, lo:lo + pair_width] for j in range(KB)]
        values = [kv_refs[j][0, :, model_width + lo:model_width + lo + pair_width] for j in range(KB)]
        outs = []
        for half in range(2):
            keep = first_half if half == 0 else jnp.logical_not(first_half)
            query_head = jnp.where(keep, query_pair, jnp.zeros_like(query_pair))
            scores = jnp.concatenate(
                [
                    lax.dot_general(
                        query_head, keys[j], (((1,), (1,)), ((), ())),
                        preferred_element_type=jnp.float32,
                    )
                    for j in range(KB)
                ],
                axis=1,
            ) * jnp.float32(HEAD_DIM ** (-0.5))
            scores = jnp.where(usable, scores, jnp.float32(-1e30))
            row_max = jnp.max(scores, axis=1, keepdims=True)
            exponent = jnp.exp(scores - row_max)
            inverse = 1.0 / jnp.sum(exponent, axis=1, keepdims=True)
            weights = exponent.astype(jnp.bfloat16)
            mixture = jnp.zeros((TILE, pair_width), jnp.float32)
            for j in range(KB):
                mixture = mixture + jnp.dot(
                    weights[:, j * TILE:(j + 1) * TILE], values[j],
                    preferred_element_type=jnp.float32,
                )
            mixture = mixture * inverse
            outs.append(mixture)
        joined = jnp.where(first_half, outs[0], outs[1])
        out_ref[:, lo:lo + pair_width] = joined.astype(out_ref.dtype)


def attend(query, kv_table, slot_index, live_mine):
    row_count, model_width = query.shape
    tile_count = row_count // TILE

    def kv_spec(j):
        return pl.BlockSpec(
            (1, TILE, 2 * model_width), lambda t, idx, live: (idx[t * KB + j], 0, 0)
        )

    grid_spec = pltpu.PrefetchScalarGridSpec(
        num_scalar_prefetch=2,
        grid=(tile_count,),
        in_specs=[pl.BlockSpec((TILE, model_width), lambda t, idx, live: (t, 0))]
        + [kv_spec(j) for j in range(KB)],
        out_specs=pl.BlockSpec((TILE, model_width), lambda t, idx, live: (t, 0)),
    )
    return pl.pallas_call(
        attention_kernel,
        grid_spec=grid_spec,
        out_shape=jax.ShapeDtypeStruct((row_count, model_width), jnp.bfloat16),
        compiler_params=pltpu.CompilerParams(dimension_semantics=("arbitrary",)),
    )(slot_index, live_mine, query, *([kv_table] * KB))


def pick_partner(bit_choice, bit_count, value):
    candidates = [partner(value, "rep", bit_number) for bit_number in range(bit_count)]
    return jax.tree.map(
        lambda *parts: lax.select_n(bit_choice, *parts) if len(parts) > 1 else parts[0],
        *candidates,
    )


def snake_ring(mesh):
    row = list(mesh.devices.reshape(-1, mesh.shape["shard"])[0])
    count = len(row)
    try:
        places = [(int(d.coords[2]), int(d.coords[0])) for d in row]
        depths = sorted({p[0] for p in places})
        widths = sorted({p[1] for p in places})
        where = {p: i for i, p in enumerate(places)}
        order = [where[(z, widths[0])] for z in depths]
        for step, z in enumerate(reversed(depths)):
            across = widths[1:] if step % 2 == 0 else widths[:0:-1]
            order.extend(where[(z, x)] for x in across)
        if sorted(order) == list(range(count)):
            return order
    except Exception:
        pass
    return list(range(count))


def ring_gather(block, ring):
    count = len(ring)
    ring_at = jnp.array(ring, jnp.int32)
    place_of = jnp.array([ring.index(i) for i in range(count)], jnp.int32)
    me = lax.axis_index("shard")
    place = place_of[me]
    ahead = [(ring[i], ring[(i + 1) % count]) for i in range(count)]
    behind = [(ring[i], ring[(i - 1) % count]) for i in range(count)]
    full = jnp.zeros((count,) + block.shape, block.dtype)
    full = lax.dynamic_update_index_in_dim(full, block, me, 0)
    forward = block
    backward = block
    for step in range(1, count // 2 + 1):
        forward = lax.ppermute(forward, "shard", ahead)
        full = lax.dynamic_update_index_in_dim(full, forward, ring_at[(place - step) % count], 0)
        if step <= (count - 1) // 2:
            backward = lax.ppermute(backward, "shard", behind)
            full = lax.dynamic_update_index_in_dim(
                full, backward, ring_at[(place + step) % count], 0
            )
    return full.reshape((count * block.shape[0],) + block.shape[1:])


def body(
    ring, cell_features, upstream, qkv_weight, out_weight, momentum, key_tiles, live_blocks, step_index
):
    features = cell_features[0]
    row_count, model_width = features.shape
    tile_count = row_count // TILE
    shard_count = lax.axis_size("shard")
    my_index = lax.axis_index("shard")
    slot_count = tile_count * KB
    remote_count = slot_count - slot_count // 2
    capacity = (remote_count + shard_count - 2) // (shard_count - 1)
    requests = key_tiles[0].reshape(shard_count, slot_count)
    owners = requests // tile_count
    local_tile = requests % tile_count
    positions = jnp.arange(slot_count, dtype=jnp.int32)
    earlier = positions[None, :] < positions[:, None]
    same_owner = owners[:, :, None] == owners[:, None, :]
    owner_rank = jnp.sum((same_owner & earlier[None]).astype(jnp.int32), axis=2)
    offsets = jnp.arange(1, shard_count, dtype=jnp.int32)
    receivers = (my_index + offsets) % shard_count
    their_owners = owners[receivers]
    their_ranks = owner_rank[receivers]
    their_local = local_tile[receivers]
    slot_ids = jnp.arange(capacity, dtype=jnp.int32)
    chosen = ((their_owners == my_index)[:, :, None]) & (their_ranks[:, :, None] == slot_ids[None, None, :])
    send_index = jnp.sum(chosen.astype(jnp.int32) * their_local[:, :, None], axis=1)
    feature_tiles = features.reshape(tile_count, TILE, model_width)
    outgoing = feature_tiles[send_index.reshape(-1)].reshape(
        shard_count - 1, capacity, TILE, model_width
    )
    arrived = [
        lax.ppermute(
            outgoing[k - 1],
            "shard",
            [(i, (i + k) % shard_count) for i in range(shard_count)],
        )
        for k in range(1, shard_count)
    ]
    arrived_rows = jnp.concatenate(arrived, axis=0).reshape(-1, model_width)
    bit_count = lax.axis_size("rep").bit_length() - 1
    bit_choice = step_index % bit_count
    own_weight = out_weight[0]
    own_moment = momentum[0]
    their_weight, their_moment = pick_partner(bit_choice, bit_count, (own_weight, own_moment))
    arrived_rows, their_weight, their_moment = lax.optimization_barrier(
        (arrived_rows, their_weight, their_moment)
    )
    my_owners = lax.dynamic_index_in_dim(owners, my_index, 0, keepdims=False)
    my_ranks = lax.dynamic_index_in_dim(owner_rank, my_index, 0, keepdims=False)
    my_local = lax.dynamic_index_in_dim(local_tile, my_index, 0, keepdims=False)
    my_remote = my_owners != my_index
    my_offset = (my_index - my_owners) % shard_count
    table_size = tile_count + (shard_count - 1) * capacity
    slot_index = jnp.where(my_remote, tile_count + (my_offset - 1) * capacity + my_ranks, my_local)
    slot_index = jnp.clip(slot_index, 0, table_size - 1).astype(jnp.int32)
    full_qkv = ring_gather(qkv_weight[0], ring)
    own_rows, full_qkv = lax.optimization_barrier((out_weight[0], full_qkv))
    query = add_rows(features, full_qkv[:, :model_width]).astype(jnp.bfloat16)
    kv_table = add_rows(
        jnp.concatenate([features, arrived_rows], axis=0), full_qkv[:, model_width:]
    ).astype(jnp.bfloat16).reshape(table_size, TILE, 2 * model_width)
    live_mine = lax.dynamic_slice_in_dim(live_blocks[0], my_index * tile_count, tile_count, 0)
    attended = attend(query, kv_table, slot_index, live_mine.astype(jnp.int32))
    product = add_rows(attended, lax.all_gather(own_rows, "shard", axis=0, tiled=True))
    layer_out = (features.astype(jnp.float32) + product).astype(jnp.bfloat16)
    partial = lax.dot_general(
        attended, upstream[0], (((0,), (0,)), ((), ())), preferred_element_type=jnp.float32
    ).astype(jnp.bfloat16)
    block_rows = partial.shape[0] // shard_count
    blocks = partial.reshape(shard_count, block_rows, partial.shape[1])
    gradient = lax.dynamic_index_in_dim(blocks, my_index, 0, keepdims=False).astype(jnp.float32)
    for k in range(1, shard_count):
        piece = lax.dynamic_index_in_dim(blocks, (my_index + k) % shard_count, 0, keepdims=False)
        received = lax.ppermute(
            piece, "shard", [(i, (i + k) % shard_count) for i in range(shard_count)]
        )
        if k == 1:
            received, layer_out = lax.optimization_barrier((received, layer_out))
        gradient = gradient + received.astype(jnp.float32)
    learn_rate = jnp.float32(50.0) / (jnp.float32(500.0) + step_index.astype(jnp.float32))
    their_gradient = pick_partner(bit_choice, bit_count, gradient.astype(jnp.bfloat16))
    velocity = momentum_beta * own_moment + gradient
    their_velocity = momentum_beta * their_moment + their_gradient.astype(jnp.float32)
    stepped = (own_weight.astype(jnp.float32) - learn_rate * velocity).astype(jnp.bfloat16)
    their_stepped = (
        their_weight.astype(jnp.float32) - learn_rate * their_velocity
    ).astype(jnp.bfloat16)
    new_weight = (
        0.5 * (stepped.astype(jnp.float32) + their_stepped.astype(jnp.float32))
    ).astype(jnp.bfloat16)
    new_momentum = 0.5 * (velocity + their_velocity)
    return (layer_out[None], new_weight[None], new_momentum[None])


def solution(mesh):
    placed = (
        P("rep", "shard", None),
        P("rep", "shard", None),
        P("rep", "shard", None),
        P("rep", "shard", None),
        P("rep", "shard", None),
        P("rep", None, None),
        P("rep", None),
        P(),
    )
    return jax.shard_map(
        functools.partial(body, snake_ring(mesh)),
        mesh=mesh,
        in_specs=placed,
        out_specs=(P("rep", "shard", None), P("rep", "shard", None), P("rep", "shard", None)),
        check_vma=False,
    )
```

```python
import functools

import jax
import jax.numpy as jnp
from jax import lax
from jax.experimental import pallas as pl
from jax.experimental.pallas import tpu as pltpu
from jax.sharding import PartitionSpec as P

HEADS = 16
HEAD_DIM = 64
TILE = 128
KB = 6


momentum_beta = 0.9


def shortened(value):

    def short(part):
        return part.astype(jnp.bfloat16) if part.dtype == jnp.float32 else part

    return jax.tree.map(short, value)


def partner(value, axis, bit):
    return lax.ppermute(value, axis, [(i, i ^ 1 << bit) for i in range(lax.axis_size(axis))])


def add_rows(source, shard_rows):
    return jnp.dot(source, shard_rows, preferred_element_type=jnp.float32)


def attention_kernel(index_ref, live_ref, query_ref, *refs):
    kv_refs = refs[:KB]
    out_ref = refs[KB]
    tile = pl.program_id(0)
    live = live_ref[tile]
    model_width = query_ref.shape[1]
    pair_width = 2 * HEAD_DIM
    lane = lax.broadcasted_iota(jnp.int32, (TILE, pair_width), 1)
    first_half = lane < HEAD_DIM
    slot_of = lax.broadcasted_iota(jnp.int32, (TILE, KB * TILE), 1) // TILE
    usable = slot_of < live
    for pair in range(HEADS // 2):
        lo = pair * pair_width
        query_pair = query_ref[:, lo:lo + pair_width]
        keys = [kv_refs[j][0, :, lo:lo + pair_width] for j in range(KB)]
        values = [kv_refs[j][0, :, model_width + lo:model_width + lo + pair_width] for j in range(KB)]
        outs = []
        for half in range(2):
            keep = first_half if half == 0 else jnp.logical_not(first_half)
            query_head = jnp.where(keep, query_pair, jnp.zeros_like(query_pair))
            scores = jnp.concatenate(
                [
                    lax.dot_general(
                        query_head, keys[j], (((1,), (1,)), ((), ())),
                        preferred_element_type=jnp.float32,
                    )
                    for j in range(KB)
                ],
                axis=1,
            ) * jnp.float32(HEAD_DIM ** (-0.5))
            scores = jnp.where(usable, scores, jnp.float32(-1e30))
            row_max = jnp.max(scores, axis=1, keepdims=True)
            exponent = jnp.exp(scores - row_max)
            inverse = 1.0 / jnp.sum(exponent, axis=1, keepdims=True)
            weights = exponent.astype(jnp.bfloat16)
            mixture = jnp.zeros((TILE, pair_width), jnp.float32)
            for j in range(KB):
                mixture = mixture + jnp.dot(
                    weights[:, j * TILE:(j + 1) * TILE], values[j],
                    preferred_element_type=jnp.float32,
                )
            mixture = mixture * inverse
            outs.append(mixture)
        joined = jnp.where(first_half, outs[0], outs[1])
        out_ref[:, lo:lo + pair_width] = joined.astype(out_ref.dtype)


def attend(query, kv_table, slot_index, live_mine):
    row_count, model_width = query.shape
    tile_count = row_count // TILE

    def kv_spec(j):
        return pl.BlockSpec(
            (1, TILE, 2 * model_width), lambda t, idx, live: (idx[t * KB + j], 0, 0)
        )

    grid_spec = pltpu.PrefetchScalarGridSpec(
        num_scalar_prefetch=2,
        grid=(tile_count,),
        in_specs=[pl.BlockSpec((TILE, model_width), lambda t, idx, live: (t, 0))]
        + [kv_spec(j) for j in range(KB)],
        out_specs=pl.BlockSpec((TILE, model_width), lambda t, idx, live: (t, 0)),
    )
    return pl.pallas_call(
        attention_kernel,
        grid_spec=grid_spec,
        out_shape=jax.ShapeDtypeStruct((row_count, model_width), jnp.bfloat16),
        compiler_params=pltpu.CompilerParams(dimension_semantics=("arbitrary",)),
    )(slot_index, live_mine, query, *([kv_table] * KB))


def pick_partner(bit_choice, bit_count, value):
    candidates = [partner(value, "rep", bit_number) for bit_number in range(bit_count)]
    return jax.tree.map(
        lambda *parts: lax.select_n(bit_choice, *parts) if len(parts) > 1 else parts[0],
        *candidates,
    )


def snake_ring(mesh):
    row = list(mesh.devices.reshape(-1, mesh.shape["shard"])[0])
    count = len(row)
    try:
        places = [(int(d.coords[2]), int(d.coords[0])) for d in row]
        depths = sorted({p[0] for p in places})
        widths = sorted({p[1] for p in places})
        where = {p: i for i, p in enumerate(places)}
        order = [where[(z, widths[0])] for z in depths]
        for step, z in enumerate(reversed(depths)):
            across = widths[1:] if step % 2 == 0 else widths[:0:-1]
            order.extend(where[(z, x)] for x in across)
        if sorted(order) == list(range(count)):
            return order
    except Exception:
        pass
    return list(range(count))


def ring_gather(block, ring, rows):
    count = len(ring)
    ring_at = jnp.array(ring, jnp.int32)
    place_of = jnp.array([ring.index(i) for i in range(count)], jnp.int32)
    me = lax.axis_index("shard")
    place = place_of[me]
    ahead = [(ring[i], ring[(i + 1) % count]) for i in range(count)]
    behind = [(ring[i], ring[(i - 1) % count]) for i in range(count)]
    width = block.shape[0]

    def product(source, piece):
        columns = lax.dynamic_slice_in_dim(rows, source * width, width, 1)
        return jnp.dot(columns, piece, preferred_element_type=jnp.float32)

    full = jnp.zeros((count,) + block.shape, block.dtype)
    full = lax.dynamic_update_index_in_dim(full, block, me, 0)
    total = product(me, block)
    forward = block
    backward = block
    for step in range(1, count // 2 + 1):
        forward = lax.ppermute(forward, "shard", ahead)
        source = ring_at[(place - step) % count]
        full = lax.dynamic_update_index_in_dim(full, forward, source, 0)
        total = total + product(source, forward)
        if step <= (count - 1) // 2:
            backward = lax.ppermute(backward, "shard", behind)
            source = ring_at[(place + step) % count]
            full = lax.dynamic_update_index_in_dim(full, backward, source, 0)
            total = total + product(source, backward)
    return full.reshape((count * width,) + block.shape[1:]), total


def body(
    ring, cell_features, upstream, qkv_weight, out_weight, momentum, key_tiles, live_blocks, step_index
):
    features = cell_features[0]
    row_count, model_width = features.shape
    tile_count = row_count // TILE
    shard_count = lax.axis_size("shard")
    my_index = lax.axis_index("shard")
    slot_count = tile_count * KB
    remote_count = slot_count - slot_count // 2
    capacity = (remote_count + shard_count - 2) // (shard_count - 1)
    requests = key_tiles[0].reshape(shard_count, slot_count)
    owners = requests // tile_count
    local_tile = requests % tile_count
    positions = jnp.arange(slot_count, dtype=jnp.int32)
    earlier = positions[None, :] < positions[:, None]
    same_owner = owners[:, :, None] == owners[:, None, :]
    owner_rank = jnp.sum((same_owner & earlier[None]).astype(jnp.int32), axis=2)
    offsets = jnp.arange(1, shard_count, dtype=jnp.int32)
    receivers = (my_index + offsets) % shard_count
    their_owners = owners[receivers]
    their_ranks = owner_rank[receivers]
    their_local = local_tile[receivers]
    slot_ids = jnp.arange(capacity, dtype=jnp.int32)
    chosen = ((their_owners == my_index)[:, :, None]) & (their_ranks[:, :, None] == slot_ids[None, None, :])
    send_index = jnp.sum(chosen.astype(jnp.int32) * their_local[:, :, None], axis=1)
    feature_tiles = features.reshape(tile_count, TILE, model_width)
    outgoing = feature_tiles[send_index.reshape(-1)].reshape(
        shard_count - 1, capacity, TILE, model_width
    )
    arrived = [
        lax.ppermute(
            outgoing[k - 1],
            "shard",
            [(i, (i + k) % shard_count) for i in range(shard_count)],
        )
        for k in range(1, shard_count)
    ]
    arrived_rows = jnp.concatenate(arrived, axis=0).reshape(-1, model_width)
    bit_count = lax.axis_size("rep").bit_length() - 1
    bit_choice = step_index % bit_count
    own_weight = out_weight[0]
    own_moment = momentum[0]
    their_weight, their_moment = pick_partner(bit_choice, bit_count, (own_weight, own_moment))
    arrived_rows, their_weight, their_moment = lax.optimization_barrier(
        (arrived_rows, their_weight, their_moment)
    )
    my_owners = lax.dynamic_index_in_dim(owners, my_index, 0, keepdims=False)
    my_ranks = lax.dynamic_index_in_dim(owner_rank, my_index, 0, keepdims=False)
    my_local = lax.dynamic_index_in_dim(local_tile, my_index, 0, keepdims=False)
    my_remote = my_owners != my_index
    my_offset = (my_index - my_owners) % shard_count
    table_size = tile_count + (shard_count - 1) * capacity
    slot_index = jnp.where(my_remote, tile_count + (my_offset - 1) * capacity + my_ranks, my_local)
    slot_index = jnp.clip(slot_index, 0, table_size - 1).astype(jnp.int32)
    full_qkv, local_projected = ring_gather(qkv_weight[0], ring, features)
    own_rows, full_qkv = lax.optimization_barrier((out_weight[0], full_qkv))
    local_projected = local_projected.astype(jnp.bfloat16)
    query = local_projected[:, :model_width]
    remote_kv = add_rows(arrived_rows, full_qkv[:, model_width:]).astype(jnp.bfloat16)
    kv_table = jnp.concatenate([local_projected[:, model_width:], remote_kv], axis=0).reshape(
        table_size, TILE, 2 * model_width
    )
    live_mine = lax.dynamic_slice_in_dim(live_blocks[0], my_index * tile_count, tile_count, 0)
    attended = attend(query, kv_table, slot_index, live_mine.astype(jnp.int32))
    product = add_rows(attended, lax.all_gather(own_rows, "shard", axis=0, tiled=True))
    layer_out = (features.astype(jnp.float32) + product).astype(jnp.bfloat16)
    partial = lax.dot_general(
        attended, upstream[0], (((0,), (0,)), ((), ())), preferred_element_type=jnp.float32
    ).astype(jnp.bfloat16)
    block_rows = partial.shape[0] // shard_count
    blocks = partial.reshape(shard_count, block_rows, partial.shape[1])
    gradient = lax.dynamic_index_in_dim(blocks, my_index, 0, keepdims=False).astype(jnp.float32)
    for k in range(1, shard_count):
        piece = lax.dynamic_index_in_dim(blocks, (my_index + k) % shard_count, 0, keepdims=False)
        received = lax.ppermute(
            piece, "shard", [(i, (i + k) % shard_count) for i in range(shard_count)]
        )
        if k == 1:
            received, layer_out = lax.optimization_barrier((received, layer_out))
        gradient = gradient + received.astype(jnp.float32)
    learn_rate = jnp.float32(50.0) / (jnp.float32(500.0) + step_index.astype(jnp.float32))
    their_gradient = pick_partner(bit_choice, bit_count, gradient.astype(jnp.bfloat16))
    velocity = momentum_beta * own_moment + gradient
    their_velocity = momentum_beta * their_moment + their_gradient.astype(jnp.float32)
    stepped = (own_weight.astype(jnp.float32) - learn_rate * velocity).astype(jnp.bfloat16)
    their_stepped = (
        their_weight.astype(jnp.float32) - learn_rate * their_velocity
    ).astype(jnp.bfloat16)
    new_weight = (
        0.5 * (stepped.astype(jnp.float32) + their_stepped.astype(jnp.float32))
    ).astype(jnp.bfloat16)
    new_momentum = 0.5 * (velocity + their_velocity)
    return (layer_out[None], new_weight[None], new_momentum[None])


def solution(mesh):
    placed = (
        P("rep", "shard", None),
        P("rep", "shard", None),
        P("rep", "shard", None),
        P("rep", "shard", None),
        P("rep", "shard", None),
        P("rep", None, None),
        P("rep", None),
        P(),
    )
    return jax.shard_map(
        functools.partial(body, snake_ring(mesh)),
        mesh=mesh,
        in_specs=placed,
        out_specs=(P("rep", "shard", None), P("rep", "shard", None), P("rep", "shard", None)),
        check_vma=False,
    )
```

```python
import functools

import jax
import jax.numpy as jnp
from jax import lax
from jax.experimental import pallas as pl
from jax.experimental.pallas import tpu as pltpu
from jax.sharding import PartitionSpec as P

HEADS = 16
HEAD_DIM = 64
TILE = 128
KB = 6


momentum_beta = 0.9


def shortened(value):

    def short(part):
        return part.astype(jnp.bfloat16) if part.dtype == jnp.float32 else part

    return jax.tree.map(short, value)


def partner(value, axis, bit):
    return lax.ppermute(value, axis, [(i, i ^ 1 << bit) for i in range(lax.axis_size(axis))])


def add_rows(source, shard_rows):
    return jnp.dot(source, shard_rows, preferred_element_type=jnp.float32)


def attention_kernel(index_ref, live_ref, query_ref, *refs):
    kv_refs = refs[:KB]
    out_ref = refs[KB]
    tile = pl.program_id(0)
    live = live_ref[tile]
    model_width = query_ref.shape[1]
    pair_width = 2 * HEAD_DIM
    lane = lax.broadcasted_iota(jnp.int32, (TILE, pair_width), 1)
    first_half = lane < HEAD_DIM
    slot_of = lax.broadcasted_iota(jnp.int32, (TILE, KB * TILE), 1) // TILE
    usable = slot_of < live
    for pair in range(HEADS // 2):
        lo = pair * pair_width
        query_pair = query_ref[:, lo:lo + pair_width]
        keys = [kv_refs[j][0, :, lo:lo + pair_width] for j in range(KB)]
        values = [kv_refs[j][0, :, model_width + lo:model_width + lo + pair_width] for j in range(KB)]
        outs = []
        for half in range(2):
            keep = first_half if half == 0 else jnp.logical_not(first_half)
            query_head = jnp.where(keep, query_pair, jnp.zeros_like(query_pair))
            scores = jnp.concatenate(
                [
                    lax.dot_general(
                        query_head, keys[j], (((1,), (1,)), ((), ())),
                        preferred_element_type=jnp.float32,
                    )
                    for j in range(KB)
                ],
                axis=1,
            ) * jnp.float32(HEAD_DIM ** (-0.5))
            scores = jnp.where(usable, scores, jnp.float32(-1e30))
            row_max = jnp.max(scores, axis=1, keepdims=True)
            exponent = jnp.exp(scores - row_max)
            inverse = 1.0 / jnp.sum(exponent, axis=1, keepdims=True)
            weights = exponent.astype(jnp.bfloat16)
            mixture = jnp.zeros((TILE, pair_width), jnp.float32)
            for j in range(KB):
                mixture = mixture + jnp.dot(
                    weights[:, j * TILE:(j + 1) * TILE], values[j],
                    preferred_element_type=jnp.float32,
                )
            mixture = mixture * inverse
            outs.append(mixture)
        joined = jnp.where(first_half, outs[0], outs[1])
        out_ref[:, lo:lo + pair_width] = joined.astype(out_ref.dtype)


def attend(query, kv_table, slot_index, live_mine):
    row_count, model_width = query.shape
    tile_count = row_count // TILE

    def kv_spec(j):
        return pl.BlockSpec(
            (1, TILE, 2 * model_width), lambda t, idx, live: (idx[t * KB + j], 0, 0)
        )

    grid_spec = pltpu.PrefetchScalarGridSpec(
        num_scalar_prefetch=2,
        grid=(tile_count,),
        in_specs=[pl.BlockSpec((TILE, model_width), lambda t, idx, live: (t, 0))]
        + [kv_spec(j) for j in range(KB)],
        out_specs=pl.BlockSpec((TILE, model_width), lambda t, idx, live: (t, 0)),
    )
    return pl.pallas_call(
        attention_kernel,
        grid_spec=grid_spec,
        out_shape=jax.ShapeDtypeStruct((row_count, model_width), jnp.bfloat16),
        compiler_params=pltpu.CompilerParams(dimension_semantics=("arbitrary",)),
    )(slot_index, live_mine, query, *([kv_table] * KB))


def pick_partner(bit_choice, bit_count, value):
    candidates = [partner(value, "rep", bit_number) for bit_number in range(bit_count)]
    return jax.tree.map(
        lambda *parts: lax.select_n(bit_choice, *parts) if len(parts) > 1 else parts[0],
        *candidates,
    )


def snake_ring(mesh):
    row = list(mesh.devices.reshape(-1, mesh.shape["shard"])[0])
    count = len(row)
    try:
        places = [(int(d.coords[2]), int(d.coords[0])) for d in row]
        depths = sorted({p[0] for p in places})
        widths = sorted({p[1] for p in places})
        where = {p: i for i, p in enumerate(places)}
        order = [where[(z, widths[0])] for z in depths]
        for step, z in enumerate(reversed(depths)):
            across = widths[1:] if step % 2 == 0 else widths[:0:-1]
            order.extend(where[(z, x)] for x in across)
        if sorted(order) == list(range(count)):
            return order
    except Exception:
        pass
    return list(range(count))


def ring_gather(block, ring, hold, hold_after):
    count = len(ring)
    ring_at = jnp.array(ring, jnp.int32)
    place_of = jnp.array([ring.index(i) for i in range(count)], jnp.int32)
    me = lax.axis_index("shard")
    place = place_of[me]
    ahead = [(ring[i], ring[(i + 1) % count]) for i in range(count)]
    behind = [(ring[i], ring[(i - 1) % count]) for i in range(count)]
    full = jnp.zeros((count,) + block.shape, block.dtype)
    full = lax.dynamic_update_index_in_dim(full, block, me, 0)
    forward = block
    backward = block
    for step in range(1, count // 2 + 1):
        forward = lax.ppermute(forward, "shard", ahead)
        full = lax.dynamic_update_index_in_dim(full, forward, ring_at[(place - step) % count], 0)
        if step <= (count - 1) // 2:
            backward = lax.ppermute(backward, "shard", behind)
            full = lax.dynamic_update_index_in_dim(
                full, backward, ring_at[(place + step) % count], 0
            )
        if step == hold_after:
            hold, forward, backward = lax.optimization_barrier((hold, forward, backward))
    return full.reshape((count * block.shape[0],) + block.shape[1:]), hold


def body(
    ring, cell_features, upstream, qkv_weight, out_weight, momentum, key_tiles, live_blocks, step_index
):
    features = cell_features[0]
    row_count, model_width = features.shape
    tile_count = row_count // TILE
    shard_count = lax.axis_size("shard")
    my_index = lax.axis_index("shard")
    slot_count = tile_count * KB
    remote_count = slot_count - slot_count // 2
    capacity = (remote_count + shard_count - 2) // (shard_count - 1)
    requests = key_tiles[0].reshape(shard_count, slot_count)
    owners = requests // tile_count
    local_tile = requests % tile_count
    positions = jnp.arange(slot_count, dtype=jnp.int32)
    earlier = positions[None, :] < positions[:, None]
    same_owner = owners[:, :, None] == owners[:, None, :]
    owner_rank = jnp.sum((same_owner & earlier[None]).astype(jnp.int32), axis=2)
    offsets = jnp.arange(1, shard_count, dtype=jnp.int32)
    receivers = (my_index + offsets) % shard_count
    their_owners = owners[receivers]
    their_ranks = owner_rank[receivers]
    their_local = local_tile[receivers]
    slot_ids = jnp.arange(capacity, dtype=jnp.int32)
    chosen = ((their_owners == my_index)[:, :, None]) & (their_ranks[:, :, None] == slot_ids[None, None, :])
    send_index = jnp.sum(chosen.astype(jnp.int32) * their_local[:, :, None], axis=1)
    feature_tiles = features.reshape(tile_count, TILE, model_width)
    outgoing = feature_tiles[send_index.reshape(-1)].reshape(
        shard_count - 1, capacity, TILE, model_width
    )
    full_qkv, outgoing = ring_gather(qkv_weight[0], ring, outgoing, 2)
    arrived = [
        lax.ppermute(
            outgoing[k - 1],
            "shard",
            [(i, (i + k) % shard_count) for i in range(shard_count)],
        )
        for k in range(1, shard_count)
    ]
    arrived_rows = jnp.concatenate(arrived, axis=0).reshape(-1, model_width)
    bit_count = lax.axis_size("rep").bit_length() - 1
    bit_choice = step_index % bit_count
    own_weight = out_weight[0]
    own_moment = momentum[0]
    their_weight, their_moment = pick_partner(bit_choice, bit_count, (own_weight, own_moment))
    arrived_rows, their_weight, their_moment = lax.optimization_barrier(
        (arrived_rows, their_weight, their_moment)
    )
    my_owners = lax.dynamic_index_in_dim(owners, my_index, 0, keepdims=False)
    my_ranks = lax.dynamic_index_in_dim(owner_rank, my_index, 0, keepdims=False)
    my_local = lax.dynamic_index_in_dim(local_tile, my_index, 0, keepdims=False)
    my_remote = my_owners != my_index
    my_offset = (my_index - my_owners) % shard_count
    table_size = tile_count + (shard_count - 1) * capacity
    slot_index = jnp.where(my_remote, tile_count + (my_offset - 1) * capacity + my_ranks, my_local)
    slot_index = jnp.clip(slot_index, 0, table_size - 1).astype(jnp.int32)
    own_rows, full_qkv = lax.optimization_barrier((out_weight[0], full_qkv))
    query = add_rows(features, full_qkv[:, :model_width]).astype(jnp.bfloat16)
    kv_table = add_rows(
        jnp.concatenate([features, arrived_rows], axis=0), full_qkv[:, model_width:]
    ).astype(jnp.bfloat16).reshape(table_size, TILE, 2 * model_width)
    live_mine = lax.dynamic_slice_in_dim(live_blocks[0], my_index * tile_count, tile_count, 0)
    attended = attend(query, kv_table, slot_index, live_mine.astype(jnp.int32))
    product = add_rows(attended, lax.all_gather(own_rows, "shard", axis=0, tiled=True))
    layer_out = (features.astype(jnp.float32) + product).astype(jnp.bfloat16)
    partial = lax.dot_general(
        attended, upstream[0], (((0,), (0,)), ((), ())), preferred_element_type=jnp.float32
    ).astype(jnp.bfloat16)
    block_rows = partial.shape[0] // shard_count
    blocks = partial.reshape(shard_count, block_rows, partial.shape[1])
    gradient = lax.dynamic_index_in_dim(blocks, my_index, 0, keepdims=False).astype(jnp.float32)
    for k in range(1, shard_count):
        piece = lax.dynamic_index_in_dim(blocks, (my_index + k) % shard_count, 0, keepdims=False)
        received = lax.ppermute(
            piece, "shard", [(i, (i + k) % shard_count) for i in range(shard_count)]
        )
        if k == 1:
            received, layer_out = lax.optimization_barrier((received, layer_out))
        gradient = gradient + received.astype(jnp.float32)
    learn_rate = jnp.float32(50.0) / (jnp.float32(500.0) + step_index.astype(jnp.float32))
    their_gradient = pick_partner(bit_choice, bit_count, gradient.astype(jnp.bfloat16))
    velocity = momentum_beta * own_moment + gradient
    their_velocity = momentum_beta * their_moment + their_gradient.astype(jnp.float32)
    stepped = (own_weight.astype(jnp.float32) - learn_rate * velocity).astype(jnp.bfloat16)
    their_stepped = (
        their_weight.astype(jnp.float32) - learn_rate * their_velocity
    ).astype(jnp.bfloat16)
    new_weight = (
        0.5 * (stepped.astype(jnp.float32) + their_stepped.astype(jnp.float32))
    ).astype(jnp.bfloat16)
    new_momentum = 0.5 * (velocity + their_velocity)
    return (layer_out[None], new_weight[None], new_momentum[None])


def solution(mesh):
    placed = (
        P("rep", "shard", None),
        P("rep", "shard", None),
        P("rep", "shard", None),
        P("rep", "shard", None),
        P("rep", "shard", None),
        P("rep", None, None),
        P("rep", None),
        P(),
    )
    return jax.shard_map(
        functools.partial(body, snake_ring(mesh)),
        mesh=mesh,
        in_specs=placed,
        out_specs=(P("rep", "shard", None), P("rep", "shard", None), P("rep", "shard", None)),
        check_vma=False,
    )
```

```python
import functools

import jax
import jax.numpy as jnp
from jax import lax
from jax.experimental import pallas as pl
from jax.experimental.pallas import tpu as pltpu
from jax.sharding import PartitionSpec as P

HEADS = 16
HEAD_DIM = 64
TILE = 128
KB = 6


momentum_beta = 0.9


def shortened(value):

    def short(part):
        return part.astype(jnp.bfloat16) if part.dtype == jnp.float32 else part

    return jax.tree.map(short, value)


def partner(value, axis, bit):
    return lax.ppermute(value, axis, [(i, i ^ 1 << bit) for i in range(lax.axis_size(axis))])


def add_rows(source, shard_rows):
    return jnp.dot(source, shard_rows, preferred_element_type=jnp.float32)


def attention_kernel(index_ref, live_ref, query_ref, *refs):
    kv_refs = refs[:KB]
    out_ref = refs[KB]
    tile = pl.program_id(0)
    live = live_ref[tile]
    model_width = query_ref.shape[1]
    pair_width = 2 * HEAD_DIM
    lane = lax.broadcasted_iota(jnp.int32, (TILE, pair_width), 1)
    first_half = lane < HEAD_DIM
    slot_of = lax.broadcasted_iota(jnp.int32, (TILE, KB * TILE), 1) // TILE
    usable = slot_of < live
    for pair in range(HEADS // 2):
        lo = pair * pair_width
        query_pair = query_ref[:, lo:lo + pair_width]
        keys = [kv_refs[j][0, :, lo:lo + pair_width] for j in range(KB)]
        values = [kv_refs[j][0, :, model_width + lo:model_width + lo + pair_width] for j in range(KB)]
        outs = []
        for half in range(2):
            keep = first_half if half == 0 else jnp.logical_not(first_half)
            query_head = jnp.where(keep, query_pair, jnp.zeros_like(query_pair))
            scores = jnp.concatenate(
                [
                    lax.dot_general(
                        query_head, keys[j], (((1,), (1,)), ((), ())),
                        preferred_element_type=jnp.float32,
                    )
                    for j in range(KB)
                ],
                axis=1,
            ) * jnp.float32(HEAD_DIM ** (-0.5))
            scores = jnp.where(usable, scores, jnp.float32(-1e30))
            row_max = jnp.max(scores, axis=1, keepdims=True)
            exponent = jnp.exp(scores - row_max)
            inverse = 1.0 / jnp.sum(exponent, axis=1, keepdims=True)
            weights = exponent.astype(jnp.bfloat16)
            mixture = jnp.zeros((TILE, pair_width), jnp.float32)
            for j in range(KB):
                mixture = mixture + jnp.dot(
                    weights[:, j * TILE:(j + 1) * TILE], values[j],
                    preferred_element_type=jnp.float32,
                )
            mixture = mixture * inverse
            outs.append(mixture)
        joined = jnp.where(first_half, outs[0], outs[1])
        out_ref[:, lo:lo + pair_width] = joined.astype(out_ref.dtype)


def attend(query, kv_table, slot_index, live_mine):
    row_count, model_width = query.shape
    tile_count = row_count // TILE

    def kv_spec(j):
        return pl.BlockSpec(
            (1, TILE, 2 * model_width), lambda t, idx, live: (idx[t * KB + j], 0, 0)
        )

    grid_spec = pltpu.PrefetchScalarGridSpec(
        num_scalar_prefetch=2,
        grid=(tile_count,),
        in_specs=[pl.BlockSpec((TILE, model_width), lambda t, idx, live: (t, 0))]
        + [kv_spec(j) for j in range(KB)],
        out_specs=pl.BlockSpec((TILE, model_width), lambda t, idx, live: (t, 0)),
    )
    return pl.pallas_call(
        attention_kernel,
        grid_spec=grid_spec,
        out_shape=jax.ShapeDtypeStruct((row_count, model_width), jnp.bfloat16),
        compiler_params=pltpu.CompilerParams(dimension_semantics=("arbitrary",)),
    )(slot_index, live_mine, query, *([kv_table] * KB))


def pick_partner(bit_choice, bit_count, value):
    candidates = [partner(value, "rep", bit_number) for bit_number in range(bit_count)]
    return jax.tree.map(
        lambda *parts: lax.select_n(bit_choice, *parts) if len(parts) > 1 else parts[0],
        *candidates,
    )


def snake_ring(mesh):
    row = list(mesh.devices.reshape(-1, mesh.shape["shard"])[0])
    count = len(row)
    try:
        places = [(int(d.coords[2]), int(d.coords[0])) for d in row]
        depths = sorted({p[0] for p in places})
        widths = sorted({p[1] for p in places})
        where = {p: i for i, p in enumerate(places)}
        order = [where[(z, widths[0])] for z in depths]
        for step, z in enumerate(reversed(depths)):
            across = widths[1:] if step % 2 == 0 else widths[:0:-1]
            order.extend(where[(z, x)] for x in across)
        if sorted(order) == list(range(count)):
            return order
    except Exception:
        pass
    return list(range(count))


def ring_gather(block, ring):
    count = len(ring)
    ring_at = jnp.array(ring, jnp.int32)
    place_of = jnp.array([ring.index(i) for i in range(count)], jnp.int32)
    me = lax.axis_index("shard")
    place = place_of[me]
    ahead = [(ring[i], ring[(i + 1) % count]) for i in range(count)]
    behind = [(ring[i], ring[(i - 1) % count]) for i in range(count)]
    full = jnp.zeros((count,) + block.shape, block.dtype)
    full = lax.dynamic_update_index_in_dim(full, block, me, 0)
    forward = block
    backward = block
    for step in range(1, count // 2 + 1):
        forward = lax.ppermute(forward, "shard", ahead)
        full = lax.dynamic_update_index_in_dim(full, forward, ring_at[(place - step) % count], 0)
        if step <= (count - 1) // 2:
            backward = lax.ppermute(backward, "shard", behind)
            full = lax.dynamic_update_index_in_dim(
                full, backward, ring_at[(place + step) % count], 0
            )
    return full.reshape((count * block.shape[0],) + block.shape[1:])


def body(
    ring, cell_features, upstream, qkv_weight, out_weight, momentum, key_tiles, live_blocks, step_index
):
    features = cell_features[0]
    row_count, model_width = features.shape
    tile_count = row_count // TILE
    shard_count = lax.axis_size("shard")
    my_index = lax.axis_index("shard")
    slot_count = tile_count * KB
    remote_count = slot_count - slot_count // 2
    capacity = (remote_count + shard_count - 2) // (shard_count - 1)
    requests = key_tiles[0].reshape(shard_count, slot_count)
    owners = requests // tile_count
    local_tile = requests % tile_count
    positions = jnp.arange(slot_count, dtype=jnp.int32)
    earlier = positions[None, :] < positions[:, None]
    same_owner = owners[:, :, None] == owners[:, None, :]
    owner_rank = jnp.sum((same_owner & earlier[None]).astype(jnp.int32), axis=2)
    offsets = jnp.arange(1, shard_count, dtype=jnp.int32)
    receivers = (my_index + offsets) % shard_count
    their_owners = owners[receivers]
    their_ranks = owner_rank[receivers]
    their_local = local_tile[receivers]
    slot_ids = jnp.arange(capacity, dtype=jnp.int32)
    chosen = ((their_owners == my_index)[:, :, None]) & (their_ranks[:, :, None] == slot_ids[None, None, :])
    send_index = jnp.sum(chosen.astype(jnp.int32) * their_local[:, :, None], axis=1)
    feature_tiles = features.reshape(tile_count, TILE, model_width)
    outgoing = feature_tiles[send_index.reshape(-1)].reshape(
        shard_count - 1, capacity, TILE, model_width
    )
    arrived = [
        lax.ppermute(
            outgoing[k - 1],
            "shard",
            [(i, (i + k) % shard_count) for i in range(shard_count)],
        )
        for k in range(1, shard_count)
    ]
    arrived_rows = jnp.concatenate(arrived, axis=0).reshape(-1, model_width)
    bit_count = lax.axis_size("rep").bit_length() - 1
    bit_choice = step_index % bit_count
    my_owners = lax.dynamic_index_in_dim(owners, my_index, 0, keepdims=False)
    my_ranks = lax.dynamic_index_in_dim(owner_rank, my_index, 0, keepdims=False)
    my_local = lax.dynamic_index_in_dim(local_tile, my_index, 0, keepdims=False)
    my_remote = my_owners != my_index
    my_offset = (my_index - my_owners) % shard_count
    table_size = tile_count + (shard_count - 1) * capacity
    slot_index = jnp.where(my_remote, tile_count + (my_offset - 1) * capacity + my_ranks, my_local)
    slot_index = jnp.clip(slot_index, 0, table_size - 1).astype(jnp.int32)
    full_qkv = ring_gather(qkv_weight[0], ring)
    own_rows, own_weight, own_moment, full_qkv = lax.optimization_barrier(
        (out_weight[0], out_weight[0], momentum[0], full_qkv)
    )
    their_weight, their_moment = pick_partner(bit_choice, bit_count, (own_weight, own_moment))
    query = add_rows(features, full_qkv[:, :model_width]).astype(jnp.bfloat16)
    kv_table = add_rows(
        jnp.concatenate([features, arrived_rows], axis=0), full_qkv[:, model_width:]
    ).astype(jnp.bfloat16).reshape(table_size, TILE, 2 * model_width)
    live_mine = lax.dynamic_slice_in_dim(live_blocks[0], my_index * tile_count, tile_count, 0)
    attended = attend(query, kv_table, slot_index, live_mine.astype(jnp.int32))
    product = add_rows(attended, lax.all_gather(own_rows, "shard", axis=0, tiled=True))
    layer_out = (features.astype(jnp.float32) + product).astype(jnp.bfloat16)
    partial = lax.dot_general(
        attended, upstream[0], (((0,), (0,)), ((), ())), preferred_element_type=jnp.float32
    ).astype(jnp.bfloat16)
    block_rows = partial.shape[0] // shard_count
    blocks = partial.reshape(shard_count, block_rows, partial.shape[1])
    gradient = lax.dynamic_index_in_dim(blocks, my_index, 0, keepdims=False).astype(jnp.float32)
    for k in range(1, shard_count):
        piece = lax.dynamic_index_in_dim(blocks, (my_index + k) % shard_count, 0, keepdims=False)
        received = lax.ppermute(
            piece, "shard", [(i, (i + k) % shard_count) for i in range(shard_count)]
        )
        if k == 1:
            received, layer_out = lax.optimization_barrier((received, layer_out))
        gradient = gradient + received.astype(jnp.float32)
    learn_rate = jnp.float32(50.0) / (jnp.float32(500.0) + step_index.astype(jnp.float32))
    their_gradient = pick_partner(bit_choice, bit_count, gradient.astype(jnp.bfloat16))
    velocity = momentum_beta * own_moment + gradient
    their_velocity = momentum_beta * their_moment + their_gradient.astype(jnp.float32)
    stepped = (own_weight.astype(jnp.float32) - learn_rate * velocity).astype(jnp.bfloat16)
    their_stepped = (
        their_weight.astype(jnp.float32) - learn_rate * their_velocity
    ).astype(jnp.bfloat16)
    new_weight = (
        0.5 * (stepped.astype(jnp.float32) + their_stepped.astype(jnp.float32))
    ).astype(jnp.bfloat16)
    new_momentum = 0.5 * (velocity + their_velocity)
    return (layer_out[None], new_weight[None], new_momentum[None])


def solution(mesh):
    placed = (
        P("rep", "shard", None),
        P("rep", "shard", None),
        P("rep", "shard", None),
        P("rep", "shard", None),
        P("rep", "shard", None),
        P("rep", None, None),
        P("rep", None),
        P(),
    )
    return jax.shard_map(
        functools.partial(body, snake_ring(mesh)),
        mesh=mesh,
        in_specs=placed,
        out_specs=(P("rep", "shard", None), P("rep", "shard", None), P("rep", "shard", None)),
        check_vma=False,
    )
```

```python
import functools

import jax
import jax.numpy as jnp
from jax import lax
from jax.experimental import pallas as pl
from jax.experimental.pallas import tpu as pltpu
from jax.sharding import PartitionSpec as P

HEADS = 16
HEAD_DIM = 64
TILE = 128
KB = 6


momentum_beta = 0.9


def shortened(value):

    def short(part):
        return part.astype(jnp.bfloat16) if part.dtype == jnp.float32 else part

    return jax.tree.map(short, value)


def partner(value, axis, bit):
    return lax.ppermute(value, axis, [(i, i ^ 1 << bit) for i in range(lax.axis_size(axis))])


def add_rows(source, shard_rows):
    return jnp.dot(source, shard_rows, preferred_element_type=jnp.float32)


def attention_kernel(index_ref, live_ref, query_ref, *refs):
    kv_refs = refs[:KB]
    out_ref = refs[KB]
    tile = pl.program_id(0)
    live = live_ref[tile]
    model_width = query_ref.shape[1]
    pair_width = 2 * HEAD_DIM
    lane = lax.broadcasted_iota(jnp.int32, (TILE, pair_width), 1)
    first_half = lane < HEAD_DIM
    slot_of = lax.broadcasted_iota(jnp.int32, (TILE, KB * TILE), 1) // TILE
    usable = slot_of < live
    for pair in range(HEADS // 2):
        lo = pair * pair_width
        query_pair = query_ref[:, lo:lo + pair_width]
        keys = [kv_refs[j][0, :, lo:lo + pair_width] for j in range(KB)]
        values = [kv_refs[j][0, :, model_width + lo:model_width + lo + pair_width] for j in range(KB)]
        outs = []
        for half in range(2):
            keep = first_half if half == 0 else jnp.logical_not(first_half)
            query_head = jnp.where(keep, query_pair, jnp.zeros_like(query_pair))
            scores = jnp.concatenate(
                [
                    lax.dot_general(
                        query_head, keys[j], (((1,), (1,)), ((), ())),
                        preferred_element_type=jnp.float32,
                    )
                    for j in range(KB)
                ],
                axis=1,
            ) * jnp.float32(HEAD_DIM ** (-0.5))
            scores = jnp.where(usable, scores, jnp.float32(-1e30))
            row_max = jnp.max(scores, axis=1, keepdims=True)
            exponent = jnp.exp(scores - row_max)
            inverse = 1.0 / jnp.sum(exponent, axis=1, keepdims=True)
            weights = exponent.astype(jnp.bfloat16)
            mixture = jnp.zeros((TILE, pair_width), jnp.float32)
            for j in range(KB):
                mixture = mixture + jnp.dot(
                    weights[:, j * TILE:(j + 1) * TILE], values[j],
                    preferred_element_type=jnp.float32,
                )
            mixture = mixture * inverse
            outs.append(mixture)
        joined = jnp.where(first_half, outs[0], outs[1])
        out_ref[:, lo:lo + pair_width] = joined.astype(out_ref.dtype)


def attend(query, kv_table, slot_index, live_mine):
    row_count, model_width = query.shape
    tile_count = row_count // TILE

    def kv_spec(j):
        return pl.BlockSpec(
            (1, TILE, 2 * model_width), lambda t, idx, live: (idx[t * KB + j], 0, 0)
        )

    grid_spec = pltpu.PrefetchScalarGridSpec(
        num_scalar_prefetch=2,
        grid=(tile_count,),
        in_specs=[pl.BlockSpec((TILE, model_width), lambda t, idx, live: (t, 0))]
        + [kv_spec(j) for j in range(KB)],
        out_specs=pl.BlockSpec((TILE, model_width), lambda t, idx, live: (t, 0)),
    )
    return pl.pallas_call(
        attention_kernel,
        grid_spec=grid_spec,
        out_shape=jax.ShapeDtypeStruct((row_count, model_width), jnp.bfloat16),
        compiler_params=pltpu.CompilerParams(dimension_semantics=("arbitrary",)),
    )(slot_index, live_mine, query, *([kv_table] * KB))


def pick_partner(bit_choice, bit_count, value):
    candidates = [partner(value, "rep", bit_number) for bit_number in range(bit_count)]
    return jax.tree.map(
        lambda *parts: lax.select_n(bit_choice, *parts) if len(parts) > 1 else parts[0],
        *candidates,
    )


def snake_ring(mesh):
    row = list(mesh.devices.reshape(-1, mesh.shape["shard"])[0])
    count = len(row)
    try:
        places = [(int(d.coords[2]), int(d.coords[0])) for d in row]
        depths = sorted({p[0] for p in places})
        widths = sorted({p[1] for p in places})
        where = {p: i for i, p in enumerate(places)}
        order = [where[(z, widths[0])] for z in depths]
        for step, z in enumerate(reversed(depths)):
            across = widths[1:] if step % 2 == 0 else widths[:0:-1]
            order.extend(where[(z, x)] for x in across)
        if sorted(order) == list(range(count)):
            return order
    except Exception:
        pass
    return list(range(count))


def ring_gather(block, ring):
    count = len(ring)
    ring_at = jnp.array(ring, jnp.int32)
    place_of = jnp.array([ring.index(i) for i in range(count)], jnp.int32)
    me = lax.axis_index("shard")
    place = place_of[me]
    ahead = [(ring[i], ring[(i + 1) % count]) for i in range(count)]
    behind = [(ring[i], ring[(i - 1) % count]) for i in range(count)]
    full = jnp.zeros((count,) + block.shape, block.dtype)
    full = lax.dynamic_update_index_in_dim(full, block, me, 0)
    forward = block
    backward = block
    for step in range(1, count // 2 + 1):
        if 2 * step == count:
            half = block.shape[0] // 2
            forward = jnp.concatenate(
                [
                    lax.ppermute(forward[:half], "shard", ahead),
                    lax.ppermute(backward[half:], "shard", behind),
                ],
                axis=0,
            )
        else:
            forward = lax.ppermute(forward, "shard", ahead)
        full = lax.dynamic_update_index_in_dim(full, forward, ring_at[(place - step) % count], 0)
        if step <= (count - 1) // 2:
            backward = lax.ppermute(backward, "shard", behind)
            full = lax.dynamic_update_index_in_dim(
                full, backward, ring_at[(place + step) % count], 0
            )
    return full.reshape((count * block.shape[0],) + block.shape[1:])


def body(
    ring, cell_features, upstream, qkv_weight, out_weight, momentum, key_tiles, live_blocks, step_index
):
    features = cell_features[0]
    row_count, model_width = features.shape
    tile_count = row_count // TILE
    shard_count = lax.axis_size("shard")
    my_index = lax.axis_index("shard")
    slot_count = tile_count * KB
    remote_count = slot_count - slot_count // 2
    capacity = (remote_count + shard_count - 2) // (shard_count - 1)
    requests = key_tiles[0].reshape(shard_count, slot_count)
    owners = requests // tile_count
    local_tile = requests % tile_count
    positions = jnp.arange(slot_count, dtype=jnp.int32)
    earlier = positions[None, :] < positions[:, None]
    same_owner = owners[:, :, None] == owners[:, None, :]
    owner_rank = jnp.sum((same_owner & earlier[None]).astype(jnp.int32), axis=2)
    offsets = jnp.arange(1, shard_count, dtype=jnp.int32)
    receivers = (my_index + offsets) % shard_count
    their_owners = owners[receivers]
    their_ranks = owner_rank[receivers]
    their_local = local_tile[receivers]
    slot_ids = jnp.arange(capacity, dtype=jnp.int32)
    chosen = ((their_owners == my_index)[:, :, None]) & (their_ranks[:, :, None] == slot_ids[None, None, :])
    send_index = jnp.sum(chosen.astype(jnp.int32) * their_local[:, :, None], axis=1)
    feature_tiles = features.reshape(tile_count, TILE, model_width)
    outgoing = feature_tiles[send_index.reshape(-1)].reshape(
        shard_count - 1, capacity, TILE, model_width
    )
    arrived = [
        lax.ppermute(
            outgoing[k - 1],
            "shard",
            [(i, (i + k) % shard_count) for i in range(shard_count)],
        )
        for k in range(1, shard_count)
    ]
    arrived_rows = jnp.concatenate(arrived, axis=0).reshape(-1, model_width)
    bit_count = lax.axis_size("rep").bit_length() - 1
    bit_choice = step_index % bit_count
    my_owners = lax.dynamic_index_in_dim(owners, my_index, 0, keepdims=False)
    my_ranks = lax.dynamic_index_in_dim(owner_rank, my_index, 0, keepdims=False)
    my_local = lax.dynamic_index_in_dim(local_tile, my_index, 0, keepdims=False)
    my_remote = my_owners != my_index
    my_offset = (my_index - my_owners) % shard_count
    table_size = tile_count + (shard_count - 1) * capacity
    slot_index = jnp.where(my_remote, tile_count + (my_offset - 1) * capacity + my_ranks, my_local)
    slot_index = jnp.clip(slot_index, 0, table_size - 1).astype(jnp.int32)
    full_qkv = ring_gather(qkv_weight[0], ring)
    own_rows, own_weight, own_moment, full_qkv = lax.optimization_barrier(
        (out_weight[0], out_weight[0], momentum[0], full_qkv)
    )
    their_weight, their_moment = pick_partner(bit_choice, bit_count, (own_weight, own_moment))
    query = add_rows(features, full_qkv[:, :model_width]).astype(jnp.bfloat16)
    kv_table = add_rows(
        jnp.concatenate([features, arrived_rows], axis=0), full_qkv[:, model_width:]
    ).astype(jnp.bfloat16).reshape(table_size, TILE, 2 * model_width)
    live_mine = lax.dynamic_slice_in_dim(live_blocks[0], my_index * tile_count, tile_count, 0)
    attended = attend(query, kv_table, slot_index, live_mine.astype(jnp.int32))
    product = add_rows(attended, lax.all_gather(own_rows, "shard", axis=0, tiled=True))
    layer_out = (features.astype(jnp.float32) + product).astype(jnp.bfloat16)
    partial = lax.dot_general(
        attended, upstream[0], (((0,), (0,)), ((), ())), preferred_element_type=jnp.float32
    ).astype(jnp.bfloat16)
    block_rows = partial.shape[0] // shard_count
    blocks = partial.reshape(shard_count, block_rows, partial.shape[1])
    gradient = lax.dynamic_index_in_dim(blocks, my_index, 0, keepdims=False).astype(jnp.float32)
    for k in range(1, shard_count):
        piece = lax.dynamic_index_in_dim(blocks, (my_index + k) % shard_count, 0, keepdims=False)
        received = lax.ppermute(
            piece, "shard", [(i, (i + k) % shard_count) for i in range(shard_count)]
        )
        if k == 1:
            received, layer_out = lax.optimization_barrier((received, layer_out))
        gradient = gradient + received.astype(jnp.float32)
    learn_rate = jnp.float32(50.0) / (jnp.float32(500.0) + step_index.astype(jnp.float32))
    their_gradient = pick_partner(bit_choice, bit_count, gradient.astype(jnp.bfloat16))
    velocity = momentum_beta * own_moment + gradient
    their_velocity = momentum_beta * their_moment + their_gradient.astype(jnp.float32)
    stepped = (own_weight.astype(jnp.float32) - learn_rate * velocity).astype(jnp.bfloat16)
    their_stepped = (
        their_weight.astype(jnp.float32) - learn_rate * their_velocity
    ).astype(jnp.bfloat16)
    new_weight = (
        0.5 * (stepped.astype(jnp.float32) + their_stepped.astype(jnp.float32))
    ).astype(jnp.bfloat16)
    new_momentum = 0.5 * (velocity + their_velocity)
    return (layer_out[None], new_weight[None], new_momentum[None])


def solution(mesh):
    placed = (
        P("rep", "shard", None),
        P("rep", "shard", None),
        P("rep", "shard", None),
        P("rep", "shard", None),
        P("rep", "shard", None),
        P("rep", None, None),
        P("rep", None),
        P(),
    )
    return jax.shard_map(
        functools.partial(body, snake_ring(mesh)),
        mesh=mesh,
        in_specs=placed,
        out_specs=(P("rep", "shard", None), P("rep", "shard", None), P("rep", "shard", None)),
        check_vma=False,
    )
```

```python
import functools

import jax
import jax.numpy as jnp
from jax import lax
from jax.experimental import pallas as pl
from jax.experimental.pallas import tpu as pltpu
from jax.sharding import PartitionSpec as P

HEADS = 16
HEAD_DIM = 64
TILE = 128
KB = 6


momentum_beta = 0.9


def shortened(value):

    def short(part):
        return part.astype(jnp.bfloat16) if part.dtype == jnp.float32 else part

    return jax.tree.map(short, value)


def partner(value, axis, bit):
    return lax.ppermute(value, axis, [(i, i ^ 1 << bit) for i in range(lax.axis_size(axis))])


def add_rows(source, shard_rows):
    return jnp.dot(source, shard_rows, preferred_element_type=jnp.float32)


def attention_kernel(index_ref, live_ref, query_ref, *refs):
    kv_refs = refs[:KB]
    out_ref = refs[KB]
    tile = pl.program_id(0)
    live = live_ref[tile]
    model_width = query_ref.shape[1]
    pair_width = 2 * HEAD_DIM
    lane = lax.broadcasted_iota(jnp.int32, (TILE, pair_width), 1)
    first_half = lane < HEAD_DIM
    slot_of = lax.broadcasted_iota(jnp.int32, (TILE, KB * TILE), 1) // TILE
    usable = slot_of < live
    for pair in range(HEADS // 2):
        lo = pair * pair_width
        query_pair = query_ref[:, lo:lo + pair_width]
        keys = [kv_refs[j][0, :, lo:lo + pair_width] for j in range(KB)]
        values = [kv_refs[j][0, :, model_width + lo:model_width + lo + pair_width] for j in range(KB)]
        outs = []
        for half in range(2):
            keep = first_half if half == 0 else jnp.logical_not(first_half)
            query_head = jnp.where(keep, query_pair, jnp.zeros_like(query_pair))
            scores = jnp.concatenate(
                [
                    lax.dot_general(
                        query_head, keys[j], (((1,), (1,)), ((), ())),
                        preferred_element_type=jnp.float32,
                    )
                    for j in range(KB)
                ],
                axis=1,
            ) * jnp.float32(HEAD_DIM ** (-0.5))
            scores = jnp.where(usable, scores, jnp.float32(-1e30))
            row_max = jnp.max(scores, axis=1, keepdims=True)
            exponent = jnp.exp(scores - row_max)
            inverse = 1.0 / jnp.sum(exponent, axis=1, keepdims=True)
            weights = exponent.astype(jnp.bfloat16)
            mixture = jnp.zeros((TILE, pair_width), jnp.float32)
            for j in range(KB):
                mixture = mixture + jnp.dot(
                    weights[:, j * TILE:(j + 1) * TILE], values[j],
                    preferred_element_type=jnp.float32,
                )
            mixture = mixture * inverse
            outs.append(mixture)
        joined = jnp.where(first_half, outs[0], outs[1])
        out_ref[:, lo:lo + pair_width] = joined.astype(out_ref.dtype)


def attend(query, kv_table, slot_index, live_mine):
    row_count, model_width = query.shape
    tile_count = row_count // TILE

    def kv_spec(j):
        return pl.BlockSpec(
            (1, TILE, 2 * model_width), lambda t, idx, live: (idx[t * KB + j], 0, 0)
        )

    grid_spec = pltpu.PrefetchScalarGridSpec(
        num_scalar_prefetch=2,
        grid=(tile_count,),
        in_specs=[pl.BlockSpec((TILE, model_width), lambda t, idx, live: (t, 0))]
        + [kv_spec(j) for j in range(KB)],
        out_specs=pl.BlockSpec((TILE, model_width), lambda t, idx, live: (t, 0)),
    )
    return pl.pallas_call(
        attention_kernel,
        grid_spec=grid_spec,
        out_shape=jax.ShapeDtypeStruct((row_count, model_width), jnp.bfloat16),
        compiler_params=pltpu.CompilerParams(dimension_semantics=("arbitrary",)),
    )(slot_index, live_mine, query, *([kv_table] * KB))


def pick_partner(bit_choice, bit_count, value):
    candidates = [partner(value, "rep", bit_number) for bit_number in range(bit_count)]
    return jax.tree.map(
        lambda *parts: lax.select_n(bit_choice, *parts) if len(parts) > 1 else parts[0],
        *candidates,
    )


def snake_ring(mesh):
    row = list(mesh.devices.reshape(-1, mesh.shape["shard"])[0])
    count = len(row)
    try:
        places = [(int(d.coords[2]), int(d.coords[0])) for d in row]
        depths = sorted({p[0] for p in places})
        widths = sorted({p[1] for p in places})
        where = {p: i for i, p in enumerate(places)}
        order = [where[(z, widths[0])] for z in depths]
        for step, z in enumerate(reversed(depths)):
            across = widths[1:] if step % 2 == 0 else widths[:0:-1]
            order.extend(where[(z, x)] for x in across)
        if sorted(order) == list(range(count)):
            return order
    except Exception:
        pass
    return list(range(count))


def ring_gather(block, ring):
    count = len(ring)
    ring_at = jnp.array(ring, jnp.int32)
    place_of = jnp.array([ring.index(i) for i in range(count)], jnp.int32)
    me = lax.axis_index("shard")
    place = place_of[me]
    ahead = [(ring[i], ring[(i + 1) % count]) for i in range(count)]
    behind = [(ring[i], ring[(i - 1) % count]) for i in range(count)]
    full = jnp.zeros((count,) + block.shape, block.dtype)
    full = lax.dynamic_update_index_in_dim(full, block, me, 0)
    forward = block
    backward = block
    for step in range(1, count // 2 + 1):
        if 2 * step == count:
            half = block.shape[0] // 2
            forward = jnp.concatenate(
                [
                    lax.ppermute(forward[:half], "shard", ahead),
                    lax.ppermute(backward[half:], "shard", behind),
                ],
                axis=0,
            )
        else:
            forward = lax.ppermute(forward, "shard", ahead)
        full = lax.dynamic_update_index_in_dim(full, forward, ring_at[(place - step) % count], 0)
        if step <= (count - 1) // 2:
            backward = lax.ppermute(backward, "shard", behind)
            full = lax.dynamic_update_index_in_dim(
                full, backward, ring_at[(place + step) % count], 0
            )
    return full.reshape((count * block.shape[0],) + block.shape[1:])


def body(
    ring, cell_features, upstream, qkv_weight, out_weight, momentum, key_tiles, live_blocks, step_index
):
    features = cell_features[0]
    row_count, model_width = features.shape
    tile_count = row_count // TILE
    shard_count = lax.axis_size("shard")
    my_index = lax.axis_index("shard")
    slot_count = tile_count * KB
    remote_count = slot_count - slot_count // 2
    capacity = (remote_count + shard_count - 2) // (shard_count - 1)
    requests = key_tiles[0].reshape(shard_count, slot_count)
    owners = requests // tile_count
    local_tile = requests % tile_count
    positions = jnp.arange(slot_count, dtype=jnp.int32)
    earlier = positions[None, :] < positions[:, None]
    same_owner = owners[:, :, None] == owners[:, None, :]
    owner_rank = jnp.sum((same_owner & earlier[None]).astype(jnp.int32), axis=2)
    offsets = jnp.arange(1, shard_count, dtype=jnp.int32)
    receivers = (my_index + offsets) % shard_count
    their_owners = owners[receivers]
    their_ranks = owner_rank[receivers]
    their_local = local_tile[receivers]
    slot_ids = jnp.arange(capacity, dtype=jnp.int32)
    chosen = ((their_owners == my_index)[:, :, None]) & (their_ranks[:, :, None] == slot_ids[None, None, :])
    send_index = jnp.sum(chosen.astype(jnp.int32) * their_local[:, :, None], axis=1)
    feature_tiles = features.reshape(tile_count, TILE, model_width)
    arrived = []
    for k in range(1, shard_count):
        outgoing = jnp.stack(
            [
                lax.dynamic_index_in_dim(feature_tiles, send_index[k - 1, c], 0, keepdims=False)
                for c in range(capacity)
            ]
        )
        arrived.append(
            lax.ppermute(
                outgoing, "shard", [(i, (i + k) % shard_count) for i in range(shard_count)]
            )
        )
    arrived_rows = jnp.concatenate(arrived, axis=0).reshape(-1, model_width)
    bit_count = lax.axis_size("rep").bit_length() - 1
    bit_choice = step_index % bit_count
    my_owners = lax.dynamic_index_in_dim(owners, my_index, 0, keepdims=False)
    my_ranks = lax.dynamic_index_in_dim(owner_rank, my_index, 0, keepdims=False)
    my_local = lax.dynamic_index_in_dim(local_tile, my_index, 0, keepdims=False)
    my_remote = my_owners != my_index
    my_offset = (my_index - my_owners) % shard_count
    table_size = tile_count + (shard_count - 1) * capacity
    slot_index = jnp.where(my_remote, tile_count + (my_offset - 1) * capacity + my_ranks, my_local)
    slot_index = jnp.clip(slot_index, 0, table_size - 1).astype(jnp.int32)
    full_qkv = ring_gather(qkv_weight[0], ring)
    own_rows, own_weight, own_moment, full_qkv = lax.optimization_barrier(
        (out_weight[0], out_weight[0], momentum[0], full_qkv)
    )
    their_weight, their_moment = pick_partner(bit_choice, bit_count, (own_weight, own_moment))
    query = add_rows(features, full_qkv[:, :model_width]).astype(jnp.bfloat16)
    kv_table = add_rows(
        jnp.concatenate([features, arrived_rows], axis=0), full_qkv[:, model_width:]
    ).astype(jnp.bfloat16).reshape(table_size, TILE, 2 * model_width)
    live_mine = lax.dynamic_slice_in_dim(live_blocks[0], my_index * tile_count, tile_count, 0)
    attended = attend(query, kv_table, slot_index, live_mine.astype(jnp.int32))
    product = add_rows(attended, lax.all_gather(own_rows, "shard", axis=0, tiled=True))
    layer_out = (features.astype(jnp.float32) + product).astype(jnp.bfloat16)
    partial = lax.dot_general(
        attended, upstream[0], (((0,), (0,)), ((), ())), preferred_element_type=jnp.float32
    ).astype(jnp.bfloat16)
    block_rows = partial.shape[0] // shard_count
    blocks = partial.reshape(shard_count, block_rows, partial.shape[1])
    gradient = lax.dynamic_index_in_dim(blocks, my_index, 0, keepdims=False).astype(jnp.float32)
    for k in range(1, shard_count):
        piece = lax.dynamic_index_in_dim(blocks, (my_index + k) % shard_count, 0, keepdims=False)
        received = lax.ppermute(
            piece, "shard", [(i, (i + k) % shard_count) for i in range(shard_count)]
        )
        if k == 1:
            received, layer_out = lax.optimization_barrier((received, layer_out))
        gradient = gradient + received.astype(jnp.float32)
    learn_rate = jnp.float32(50.0) / (jnp.float32(500.0) + step_index.astype(jnp.float32))
    their_gradient = pick_partner(bit_choice, bit_count, gradient.astype(jnp.bfloat16))
    velocity = momentum_beta * own_moment + gradient
    their_velocity = momentum_beta * their_moment + their_gradient.astype(jnp.float32)
    stepped = (own_weight.astype(jnp.float32) - learn_rate * velocity).astype(jnp.bfloat16)
    their_stepped = (
        their_weight.astype(jnp.float32) - learn_rate * their_velocity
    ).astype(jnp.bfloat16)
    new_weight = (
        0.5 * (stepped.astype(jnp.float32) + their_stepped.astype(jnp.float32))
    ).astype(jnp.bfloat16)
    new_momentum = 0.5 * (velocity + their_velocity)
    return (layer_out[None], new_weight[None], new_momentum[None])


def solution(mesh):
    placed = (
        P("rep", "shard", None),
        P("rep", "shard", None),
        P("rep", "shard", None),
        P("rep", "shard", None),
        P("rep", "shard", None),
        P("rep", None, None),
        P("rep", None),
        P(),
    )
    return jax.shard_map(
        functools.partial(body, snake_ring(mesh)),
        mesh=mesh,
        in_specs=placed,
        out_specs=(P("rep", "shard", None), P("rep", "shard", None), P("rep", "shard", None)),
        check_vma=False,
    )
```

```python
import functools

import jax
import jax.numpy as jnp
from jax import lax
from jax.experimental import pallas as pl
from jax.experimental.pallas import tpu as pltpu
from jax.sharding import PartitionSpec as P

HEADS = 16
HEAD_DIM = 64
TILE = 128
KB = 6


momentum_beta = 0.9


def shortened(value):

    def short(part):
        return part.astype(jnp.bfloat16) if part.dtype == jnp.float32 else part

    return jax.tree.map(short, value)


def partner(value, axis, bit):
    return lax.ppermute(value, axis, [(i, i ^ 1 << bit) for i in range(lax.axis_size(axis))])


def add_rows(source, shard_rows):
    return jnp.dot(source, shard_rows, preferred_element_type=jnp.float32)


def attention_kernel(index_ref, live_ref, query_ref, *refs):
    key_refs = refs[:KB]
    value_refs = refs[KB:2 * KB]
    out_ref = refs[2 * KB]
    tile = pl.program_id(0)
    live = live_ref[tile]
    pair_width = 2 * HEAD_DIM
    lane = lax.broadcasted_iota(jnp.int32, (TILE, pair_width), 1)
    first_half = lane < HEAD_DIM
    slot_of = lax.broadcasted_iota(jnp.int32, (TILE, KB * TILE), 1) // TILE
    usable = slot_of < live
    for pair in range(query_ref.shape[1] // pair_width):
        lo = pair * pair_width
        query_pair = query_ref[:, lo:lo + pair_width]
        keys = [key_refs[j][0, :, lo:lo + pair_width] for j in range(KB)]
        values = [value_refs[j][0, :, lo:lo + pair_width] for j in range(KB)]
        outs = []
        for half in range(2):
            keep = first_half if half == 0 else jnp.logical_not(first_half)
            query_head = jnp.where(keep, query_pair, jnp.zeros_like(query_pair))
            scores = jnp.concatenate(
                [
                    lax.dot_general(
                        query_head, keys[j], (((1,), (1,)), ((), ())),
                        preferred_element_type=jnp.float32,
                    )
                    for j in range(KB)
                ],
                axis=1,
            ) * jnp.float32(HEAD_DIM ** (-0.5))
            scores = jnp.where(usable, scores, jnp.float32(-1e30))
            row_max = jnp.max(scores, axis=1, keepdims=True)
            exponent = jnp.exp(scores - row_max)
            inverse = 1.0 / jnp.sum(exponent, axis=1, keepdims=True)
            weights = exponent.astype(jnp.bfloat16)
            mixture = jnp.zeros((TILE, pair_width), jnp.float32)
            for j in range(KB):
                mixture = mixture + jnp.dot(
                    weights[:, j * TILE:(j + 1) * TILE], values[j],
                    preferred_element_type=jnp.float32,
                )
            mixture = mixture * inverse
            outs.append(mixture)
        joined = jnp.where(first_half, outs[0], outs[1])
        out_ref[:, lo:lo + pair_width] = joined.astype(out_ref.dtype)


def attend(query, kv_table, slot_index, live_mine):
    row_count, model_width = query.shape
    tile_count = row_count // TILE
    parts = 2
    width = model_width // parts

    def key_spec(j):
        return pl.BlockSpec(
            (1, TILE, width), lambda t, g, idx, live: (idx[t * KB + j], 0, g)
        )

    def value_spec(j):
        return pl.BlockSpec(
            (1, TILE, width), lambda t, g, idx, live: (idx[t * KB + j], 0, parts + g)
        )

    grid_spec = pltpu.PrefetchScalarGridSpec(
        num_scalar_prefetch=2,
        grid=(tile_count, parts),
        in_specs=[pl.BlockSpec((TILE, width), lambda t, g, idx, live: (t, g))]
        + [key_spec(j) for j in range(KB)]
        + [value_spec(j) for j in range(KB)],
        out_specs=pl.BlockSpec((TILE, width), lambda t, g, idx, live: (t, g)),
    )
    return pl.pallas_call(
        attention_kernel,
        grid_spec=grid_spec,
        out_shape=jax.ShapeDtypeStruct((row_count, model_width), jnp.bfloat16),
        compiler_params=pltpu.CompilerParams(dimension_semantics=("arbitrary", "arbitrary")),
    )(slot_index, live_mine, query, *([kv_table] * (2 * KB)))


def pick_partner(bit_choice, bit_count, value):
    candidates = [partner(value, "rep", bit_number) for bit_number in range(bit_count)]
    return jax.tree.map(
        lambda *parts: lax.select_n(bit_choice, *parts) if len(parts) > 1 else parts[0],
        *candidates,
    )


def snake_ring(mesh):
    row = list(mesh.devices.reshape(-1, mesh.shape["shard"])[0])
    count = len(row)
    try:
        places = [(int(d.coords[2]), int(d.coords[0])) for d in row]
        depths = sorted({p[0] for p in places})
        widths = sorted({p[1] for p in places})
        where = {p: i for i, p in enumerate(places)}
        order = [where[(z, widths[0])] for z in depths]
        for step, z in enumerate(reversed(depths)):
            across = widths[1:] if step % 2 == 0 else widths[:0:-1]
            order.extend(where[(z, x)] for x in across)
        if sorted(order) == list(range(count)):
            return order
    except Exception:
        pass
    return list(range(count))


def ring_gather(block, ring):
    count = len(ring)
    ring_at = jnp.array(ring, jnp.int32)
    place_of = jnp.array([ring.index(i) for i in range(count)], jnp.int32)
    me = lax.axis_index("shard")
    place = place_of[me]
    ahead = [(ring[i], ring[(i + 1) % count]) for i in range(count)]
    behind = [(ring[i], ring[(i - 1) % count]) for i in range(count)]
    full = jnp.zeros((count,) + block.shape, block.dtype)
    full = lax.dynamic_update_index_in_dim(full, block, me, 0)
    forward = block
    backward = block
    for step in range(1, count // 2 + 1):
        if 2 * step == count:
            half = block.shape[0] // 2
            forward = jnp.concatenate(
                [
                    lax.ppermute(forward[:half], "shard", ahead),
                    lax.ppermute(backward[half:], "shard", behind),
                ],
                axis=0,
            )
        else:
            forward = lax.ppermute(forward, "shard", ahead)
        full = lax.dynamic_update_index_in_dim(full, forward, ring_at[(place - step) % count], 0)
        if step <= (count - 1) // 2:
            backward = lax.ppermute(backward, "shard", behind)
            full = lax.dynamic_update_index_in_dim(
                full, backward, ring_at[(place + step) % count], 0
            )
    return full.reshape((count * block.shape[0],) + block.shape[1:])


def body(
    ring, cell_features, upstream, qkv_weight, out_weight, momentum, key_tiles, live_blocks, step_index
):
    features = cell_features[0]
    row_count, model_width = features.shape
    tile_count = row_count // TILE
    shard_count = lax.axis_size("shard")
    my_index = lax.axis_index("shard")
    slot_count = tile_count * KB
    remote_count = slot_count - slot_count // 2
    capacity = (remote_count + shard_count - 2) // (shard_count - 1)
    requests = key_tiles[0].reshape(shard_count, slot_count)
    owners = requests // tile_count
    local_tile = requests % tile_count
    positions = jnp.arange(slot_count, dtype=jnp.int32)
    earlier = positions[None, :] < positions[:, None]
    same_owner = owners[:, :, None] == owners[:, None, :]
    owner_rank = jnp.sum((same_owner & earlier[None]).astype(jnp.int32), axis=2)
    offsets = jnp.arange(1, shard_count, dtype=jnp.int32)
    receivers = (my_index + offsets) % shard_count
    their_owners = owners[receivers]
    their_ranks = owner_rank[receivers]
    their_local = local_tile[receivers]
    slot_ids = jnp.arange(capacity, dtype=jnp.int32)
    chosen = ((their_owners == my_index)[:, :, None]) & (their_ranks[:, :, None] == slot_ids[None, None, :])
    send_index = jnp.sum(chosen.astype(jnp.int32) * their_local[:, :, None], axis=1)
    feature_tiles = features.reshape(tile_count, TILE, model_width)
    outgoing = feature_tiles[send_index.reshape(-1)].reshape(
        shard_count - 1, capacity, TILE, model_width
    )
    arrived = [
        lax.ppermute(
            outgoing[k - 1],
            "shard",
            [(i, (i + k) % shard_count) for i in range(shard_count)],
        )
        for k in range(1, shard_count)
    ]
    arrived_rows = jnp.concatenate(arrived, axis=0).reshape(-1, model_width)
    bit_count = lax.axis_size("rep").bit_length() - 1
    bit_choice = step_index % bit_count
    my_owners = lax.dynamic_index_in_dim(owners, my_index, 0, keepdims=False)
    my_ranks = lax.dynamic_index_in_dim(owner_rank, my_index, 0, keepdims=False)
    my_local = lax.dynamic_index_in_dim(local_tile, my_index, 0, keepdims=False)
    my_remote = my_owners != my_index
    my_offset = (my_index - my_owners) % shard_count
    table_size = tile_count + (shard_count - 1) * capacity
    slot_index = jnp.where(my_remote, tile_count + (my_offset - 1) * capacity + my_ranks, my_local)
    slot_index = jnp.clip(slot_index, 0, table_size - 1).astype(jnp.int32)
    full_qkv = ring_gather(qkv_weight[0], ring)
    own_rows, own_weight, own_moment, full_qkv = lax.optimization_barrier(
        (out_weight[0], out_weight[0], momentum[0], full_qkv)
    )
    their_weight, their_moment = pick_partner(bit_choice, bit_count, (own_weight, own_moment))
    query = add_rows(features, full_qkv[:, :model_width]).astype(jnp.bfloat16)
    kv_table = add_rows(
        jnp.concatenate([features, arrived_rows], axis=0), full_qkv[:, model_width:]
    ).astype(jnp.bfloat16).reshape(table_size, TILE, 2 * model_width)
    live_mine = lax.dynamic_slice_in_dim(live_blocks[0], my_index * tile_count, tile_count, 0)
    attended = attend(query, kv_table, slot_index, live_mine.astype(jnp.int32))
    product = add_rows(attended, lax.all_gather(own_rows, "shard", axis=0, tiled=True))
    layer_out = (features.astype(jnp.float32) + product).astype(jnp.bfloat16)
    partial = lax.dot_general(
        attended, upstream[0], (((0,), (0,)), ((), ())), preferred_element_type=jnp.float32
    ).astype(jnp.bfloat16)
    block_rows = partial.shape[0] // shard_count
    blocks = partial.reshape(shard_count, block_rows, partial.shape[1])
    gradient = lax.dynamic_index_in_dim(blocks, my_index, 0, keepdims=False).astype(jnp.float32)
    for k in range(1, shard_count):
        piece = lax.dynamic_index_in_dim(blocks, (my_index + k) % shard_count, 0, keepdims=False)
        received = lax.ppermute(
            piece, "shard", [(i, (i + k) % shard_count) for i in range(shard_count)]
        )
        if k == 1:
            received, layer_out = lax.optimization_barrier((received, layer_out))
        gradient = gradient + received.astype(jnp.float32)
    learn_rate = jnp.float32(50.0) / (jnp.float32(500.0) + step_index.astype(jnp.float32))
    their_gradient = pick_partner(bit_choice, bit_count, gradient.astype(jnp.bfloat16))
    velocity = momentum_beta * own_moment + gradient
    their_velocity = momentum_beta * their_moment + their_gradient.astype(jnp.float32)
    stepped = (own_weight.astype(jnp.float32) - learn_rate * velocity).astype(jnp.bfloat16)
    their_stepped = (
        their_weight.astype(jnp.float32) - learn_rate * their_velocity
    ).astype(jnp.bfloat16)
    new_weight = (
        0.5 * (stepped.astype(jnp.float32) + their_stepped.astype(jnp.float32))
    ).astype(jnp.bfloat16)
    new_momentum = 0.5 * (velocity + their_velocity)
    return (layer_out[None], new_weight[None], new_momentum[None])


def solution(mesh):
    placed = (
        P("rep", "shard", None),
        P("rep", "shard", None),
        P("rep", "shard", None),
        P("rep", "shard", None),
        P("rep", "shard", None),
        P("rep", None, None),
        P("rep", None),
        P(),
    )
    return jax.shard_map(
        functools.partial(body, snake_ring(mesh)),
        mesh=mesh,
        in_specs=placed,
        out_specs=(P("rep", "shard", None), P("rep", "shard", None), P("rep", "shard", None)),
        check_vma=False,
    )
```
